32 devices in a mesh: grp: 4 (over z), exp: 8 (over y, x, core).
Axes of the slice: x: 2, y: 2, z: 4, core: 2. Of those that a mesh axis runs over, the one named last changes fastest.
Arguments:
- cotangent: bfloat16 [4096, 1440], P(('grp', 'exp')), may hold values from -6 to 6
- hidden: bfloat16 [4096, 4, 1440], P(('grp', 'exp')), may hold values from -0.29882812 to 0.29882812
- gates: bfloat16 [4096, 4], P(('grp', 'exp')), may hold values from 0.049804688 to 1
- expert_ids: int32 [4096, 4], P(('grp', 'exp')), may hold values from 0 to 15, all different within a row; in each aligned block of 128 rows (0 to 127, 128 to 255, ...) at most 40 rows name the same one
- group_counts: int32 [4], P('grp'), may hold values from 146 to 1024, as said below
- w_down: bfloat16 [16, 1440, 1440], P('exp', 'grp'), may hold values from -0.15625 to 0.15625
Outputs:
- d_hidden: bfloat16 [4096, 4, 1440], P(('grp', 'exp'))
- d_gate: bfloat16 [4096, 4], P(('grp', 'exp'))
- d_weight: float32 [16, 1440, 1440], P('exp', 'grp')
The draws below stay inside these ranges and needn't reach their ends.
Inputs may be any that keep to these rules, and one draw needn't show every extreme that they name: `expert_ids`: within the rows of one device no expert is named more than 40 times, and every expert is named somewhere. `group_counts`: some group has all 1024 slots live, and some group only 146.
All inputs are finite; a program needn't handle non-finite values.
Results may differ from the reference program's by a relative error of at most 0.015.
Values may be sent and summed in bfloat16 or wider, within the bound.
No kernel may reach another device: no remote copies, remote signals or barrier semaphores. Data moves between devices by JAX's collectives and lax.ppermute only.
A program may use at most 128 MiB of HBM per device.

```python
import math
import jax
import jax.numpy as jnp
import numpy as np
from jax import lax

TOP = 4
FFW = 1440
DW = 1440
TOK_DEV = 128
EXPERTS = 16
MOST = 40
LOSS_SCALE = 32768
GROUP_TOK = 1024
GROUPS = 4
TOKENS = 4096
N_EXP = 8


def draw_group_counts(key, part):
    speed_key = jax.random.fold_in(key, 11)
    order_key = jax.random.fold_in(key, 12)
    speeds = jax.random.randint(speed_key, (GROUPS,), 1, 8).astype(jnp.int32)
    order = jax.random.permutation(order_key, GROUPS)
    speeds = speeds.at[order[0]].set(7).at[order[1]].set(1)
    return speeds * GROUP_TOK // 7


def shard_levels(stream_key, dims, cuts, low, top_value):
    gain = 1.0
    for position, parts in cuts:
        steps = jax.random.uniform(jax.random.fold_in(jax.random.fold_in(stream_key, 6), position), (parts,), jnp.float32, low / len(cuts), top_value / len(cuts))
        gain = gain * jnp.repeat(jnp.exp(steps), dims[position] // parts).reshape((-1,) + (1,) * (len(dims) - 1 - position))
    return gain


def routed_block(own_key, own, number, rows, number_of, top, limit, slope):
    sequence = jax.random.permutation(own_key, number_of)
    crowded, common = portions_of(number_of, rows * top, limit, slope, True), portions_of(number_of, rows * top, limit, slope, False)
    places = jnp.arange(number_of)

    def named(sizes, offset_by):
        used = int((sizes > 0).sum())
        fixed = max(1, used // 4)
        moved = fixed + (places - fixed + offset_by * (used - fixed)) % max(1, number_of - fixed)
        return jnp.zeros((number_of,), jnp.int32).at[sequence[jnp.where(places < fixed, places, moved)]].set(jnp.asarray(sizes, jnp.int32))

    sizes = jnp.where(number % 4 == 0, named(crowded, number // 4), named(common, number - number // 4 - 1))
    mixed = jax.random.permutation(jax.random.fold_in(own, 3), number_of)
    source_of, receiver = mixed[0:number_of // 2 * 2:2], mixed[1:number_of // 2 * 2:2]
    slack = jnp.minimum(sizes[source_of] - 1, limit - sizes[receiver]) // 2
    slack = jnp.where((source_of == sequence[0]) | (receiver == sequence[0]) | (sizes[receiver] == 0), 0, jnp.maximum(slack, 0))
    moved = jax.random.randint(jax.random.fold_in(own, 4), (number_of // 2,), 0, 1 << 20) % (slack + 1)
    sizes = sizes.at[source_of].add(-moved).at[receiver].add(moved)
    items = jnp.searchsorted(jnp.cumsum(sizes), jnp.arange(rows * top), side="right").astype(jnp.int32)
    grid = items.reshape(top, rows).T
    grid = grid[jax.random.permutation(jax.random.fold_in(own, 1), rows)]
    offset_by = jax.random.randint(jax.random.fold_in(own, 2), (rows, 1), 0, top)
    return jnp.take_along_axis(grid, (jnp.arange(top)[None, :] + offset_by) % top, axis=1)


def portions_of(amount, total, limit, lean, full):
    loads = [(1 << 20) // math.isqrt(rank ** lean) + 1 for rank in range(1, amount + 1)]
    largest = limit if full else min(limit, max(-(-total // amount), total * loads[0] // sum(loads)))
    least = 1 if total - largest >= amount - 1 else 0
    given, spare = [largest] + [least] * (amount - 1), total - largest - least * (amount - 1)
    while spare > 0:
        free = [i for i in range(1, amount) if given[i] < largest] or [i for i in range(1, amount) if given[i] < limit]
        pool, budget = sum([loads[i] for i in free]), spare
        for i in free:
            more = min(limit - given[i], max(1, budget * loads[i] // pool), spare)
            given[i] = given[i] + more
            spare = spare - more
    return np.array(given)


def normal_values(stream_key, dims, deviation, most, shards=(), kind=jnp.bfloat16):
    entries = deviation * jax.random.normal(stream_key, dims, jnp.float32)
    if shards:
        entries = entries * shard_levels(stream_key, dims, shards, -0.22, 0.18)
    return jnp.clip(entries, -most, most).astype(kind)


def setup_inputs(seed: int = 0) -> dict:
    splits = jax.random.split(jax.random.key(seed), 7)
    cotangent = normal_values(splits[0], (TOKENS, DW), 1.0, 6.0, ((0, 32),))
    hidden = normal_values(splits[1], (TOKENS, TOP, FFW), 0.05, 0.29882812, ((0, 32),))
    gates = jnp.clip(0.049804688 + 0.9501953 * jax.random.uniform(splits[2], (TOKENS, TOP), jnp.float32) ** shard_levels(splits[2], (TOKENS, TOP), ((0, 32),), -0.2, 0.2), 0.049804688, 1.0).astype(jnp.bfloat16)
    expert_ids_keys = jax.random.split(jax.random.fold_in(splits[3], 1), TOKENS // TOK_DEV)
    expert_ids_turns = jax.random.permutation(jax.random.fold_in(splits[3], 3), TOKENS // TOK_DEV)
    expert_ids = jax.vmap(lambda own, number: routed_block(jax.random.fold_in(splits[3], 2), own, number, TOK_DEV, EXPERTS, TOP, MOST, 1))(expert_ids_keys, expert_ids_turns).reshape((TOKENS, TOP))
    group_counts = draw_group_counts(jax.random.fold_in(splits[6], 71), 0)
    w_down = normal_values(splits[5], (EXPERTS, FFW, DW), FFW ** -0.5, 0.15625, ((0, 8), (1, 4)))
    return {"cotangent": cotangent, "hidden": hidden, "gates": gates, "expert_ids": expert_ids, "group_counts": group_counts, "w_down": w_down}


def reference(cotangent, hidden, gates, expert_ids, group_counts, w_down):
    tokens = cotangent.shape[0]
    groups = group_counts.shape[0]
    per_group = tokens // groups
    rows = jnp.arange(tokens, dtype=jnp.int32)
    group_of = rows // per_group
    live = ((rows % per_group) < group_counts[group_of]).astype(jnp.float32)
    total = jnp.sum(group_counts.astype(jnp.float32))
    scale = LOSS_SCALE / total
    weighted = (gates.astype(jnp.float32) * live[:, None]).astype(jnp.bfloat16)
    flat_ids = expert_ids.reshape(-1)
    slots = tokens * TOP
    slot_tok = jnp.arange(slots, dtype=jnp.int32) // TOP
    hidden_flat = hidden.reshape(slots, FFW)
    weighted_flat = weighted.reshape(-1)
    capacity = groups * N_EXP * MOST

    def per_expert(expert):
        hits = flat_ids == expert
        index = jnp.nonzero(hits, size=capacity, fill_value=0)[0].astype(jnp.int32)
        count = jnp.sum(hits.astype(jnp.int32))
        used = jnp.arange(capacity, dtype=jnp.int32) < count
        tok_index = slot_tok[index]
        dy_rows = cotangent[tok_index]
        h_rows = jnp.where(used[:, None], hidden_flat[index], jnp.zeros((), jnp.bfloat16))
        g_rows = jnp.where(used, weighted_flat[index], jnp.zeros((), jnp.bfloat16))
        proj = jnp.dot(dy_rows, w_down[expert].T, preferred_element_type=jnp.float32)
        dh_rows = (g_rows.astype(jnp.float32)[:, None] * proj).astype(jnp.bfloat16)
        inner = jnp.sum(h_rows.astype(jnp.float32) * proj, axis=1).astype(jnp.bfloat16)
        scaled = (g_rows.astype(jnp.float32)[:, None] * dy_rows.astype(jnp.float32)).astype(jnp.bfloat16)
        grp_rows = group_of[tok_index]
        grad = jnp.zeros((FFW, DW), jnp.float32)
        for group in range(groups):
            mask = jnp.where(grp_rows == group, jnp.ones((), jnp.bfloat16), jnp.zeros((), jnp.bfloat16))
            part = jnp.dot((h_rows * mask[:, None]).T, scaled, preferred_element_type=jnp.float32)
            grad = grad + (part * scale).astype(jnp.bfloat16).astype(jnp.float32)
        target = jnp.where(used, index, slots)
        return dh_rows, inner, target, grad

    dh_all, inner_all, target_all, d_weight = lax.map(per_expert, jnp.arange(EXPERTS, dtype=jnp.int32))
    target_flat = target_all.reshape(-1)
    d_hidden = jnp.zeros((slots, FFW), jnp.bfloat16).at[target_flat].set(dh_all.reshape(-1, FFW), mode="drop")
    inner_flat = jnp.zeros((slots,), jnp.bfloat16).at[target_flat].set(inner_all.reshape(-1), mode="drop")
    d_gate = (inner_flat.reshape(tokens, TOP).astype(jnp.float32) * live[:, None]).astype(jnp.bfloat16)
    return d_hidden.reshape(tokens, TOP, FFW), d_gate, d_weight
```

```python
import jax
import jax.numpy as jnp
from jax import lax
from jax.sharding import PartitionSpec as P

LOSS_SCALE = 32768


def body(cotangent, hidden, gates, expert_ids, group_counts, w_down):
    tok = cotangent.shape[0]
    top = expert_ids.shape[1]
    ffw = hidden.shape[2]
    width = cotangent.shape[1]
    n_exp = lax.axis_size("exp")
    n_grp = lax.axis_size("grp")
    exp_dev = w_down.shape[0]
    experts = exp_dev * n_exp
    most = 5 * tok * top // (4 * experts)
    count = group_counts[0]
    first_row = lax.axis_index("exp") * tok
    live = (first_row + jnp.arange(tok, dtype=jnp.int32) < count).astype(jnp.float32)
    total = jnp.sum(lax.all_gather(group_counts, "grp", tiled=True).astype(jnp.float32))
    scale = LOSS_SCALE / total
    weighted = (gates.astype(jnp.float32) * live[:, None]).astype(jnp.bfloat16)
    flat_ids = expert_ids.reshape(-1)
    onehot = (flat_ids[:, None] == jnp.arange(experts, dtype=jnp.int32)[None, :]).astype(jnp.int32)
    rank = jnp.sum((jnp.cumsum(onehot, axis=0) - onehot) * onehot, axis=1)
    target = flat_ids * most + rank
    slot_tok = jnp.arange(tok * top, dtype=jnp.int32) // top
    dy_buf = jnp.zeros((experts * most, width), jnp.bfloat16).at[target].set(cotangent[slot_tok])
    hid_buf = jnp.zeros((experts * most, ffw), jnp.bfloat16).at[target].set(hidden.reshape(-1, ffw))
    gate_buf = jnp.zeros((experts * most,), jnp.bfloat16).at[target].set(weighted.reshape(-1))
    dy_buf = dy_buf.reshape(n_exp, exp_dev * most, width)
    hid_buf = hid_buf.reshape(n_exp, exp_dev * most, ffw)
    gate_buf = gate_buf.reshape(n_exp, exp_dev * most)
    dy_recv, gate_recv = (
        lax.all_to_all(dy_buf, "exp", split_axis=0, concat_axis=0, tiled=True),
        lax.all_to_all(gate_buf, "exp", split_axis=0, concat_axis=0, tiled=True),
    )
    hid_recv = lax.all_to_all(hid_buf, "exp", split_axis=0, concat_axis=0, tiled=True)
    dy_four = dy_recv.reshape(n_exp, exp_dev, most, width)
    hid_four = hid_recv.reshape(n_exp, exp_dev, most, ffw)
    gate_three = gate_recv.reshape(n_exp, exp_dev, most).astype(jnp.float32)
    proj = jnp.einsum(
        "sjmd,jfd->sjmf",
        dy_four,
        lax.all_gather(w_down, "grp", axis=1, tiled=True),
        preferred_element_type=jnp.float32,
    )
    dh_rows = (gate_three[..., None] * proj).astype(jnp.bfloat16)
    inner = jnp.sum(hid_four.astype(jnp.float32) * proj, axis=3).astype(jnp.bfloat16)
    scaled = (gate_three[..., None] * dy_four.astype(jnp.float32)).astype(jnp.bfloat16)
    partial_grad = (
        jnp.einsum(
            "sjmgf,sjmd->gjfd",
            hid_four.reshape(n_exp, exp_dev, most, n_grp, ffw // n_grp),
            scaled,
            preferred_element_type=jnp.float32,
        )
        * scale
    )
    grad_rows = partial_grad.astype(jnp.bfloat16).reshape(ffw * exp_dev, width)
    d_weight = (
        lax.psum_scatter(grad_rows, "grp", scatter_dimension=0, tiled=True)
        .reshape(exp_dev, ffw // n_grp, width)
        .astype(jnp.float32)
    )
    back_dh, back_inner = (
        lax.all_to_all(
            dh_rows.reshape(n_exp, exp_dev * most, ffw),
            "exp",
            split_axis=0,
            concat_axis=0,
            tiled=True,
        ),
        lax.all_to_all(
            inner.reshape(n_exp, exp_dev * most), "exp", split_axis=0, concat_axis=0, tiled=True
        ),
    )
    d_hidden = back_dh.reshape(experts * most, ffw)[target].reshape(tok, top, ffw)
    inner_tok = back_inner.reshape(-1)[target].reshape(tok, top)
    d_gate = (inner_tok.astype(jnp.float32) * live[:, None]).astype(jnp.bfloat16)
    return (d_hidden, d_gate, d_weight)


def solution(mesh):
    in_specs = (
        P(("grp", "exp"), None),
        P(("grp", "exp"), None, None),
        P(("grp", "exp"), None),
        P(("grp", "exp"), None),
        P("grp"),
        P("exp", "grp", None),
    )
    out_specs = (P(("grp", "exp"), None, None), P(("grp", "exp"), None), P("exp", "grp", None))
    return jax.shard_map(body, mesh=mesh, in_specs=in_specs, out_specs=out_specs, check_vma=False)
```

```python
import jax
import jax.numpy as jnp
from jax import lax
from jax.sharding import PartitionSpec as P

LOSS_SCALE = 32768


def body(cotangent, hidden, gates, expert_ids, group_counts, w_down):
    tok, top = expert_ids.shape
    ffw = hidden.shape[2]
    width = cotangent.shape[1]
    n_exp = lax.axis_size("exp")
    n_grp = lax.axis_size("grp")
    exp_dev, f_loc = w_down.shape[0], w_down.shape[1]
    experts = exp_dev * n_exp
    most = 5 * tok * top // (4 * experts)
    slots = n_grp * tok * top
    rows = n_exp * n_grp * exp_dev * most

    counts = lax.all_gather(group_counts, "grp", tiled=True)
    count = group_counts[0]
    first_row = lax.axis_index("exp") * tok
    live = (first_row + jnp.arange(tok, dtype=jnp.int32) < count).astype(jnp.float32)
    total = jnp.sum(counts.astype(jnp.float32))
    scale = LOSS_SCALE / total
    weighted = (gates.astype(jnp.float32) * live[:, None]).astype(jnp.bfloat16)

    cot_all = lax.all_gather(cotangent, "grp", tiled=True)
    ids_all = lax.all_gather(expert_ids, "grp").reshape(n_grp, tok * top)
    wt_all = lax.all_gather(weighted, "grp").reshape(slots)
    hid_split = jnp.transpose(hidden.reshape(tok, top, n_grp, f_loc), (2, 0, 1, 3))
    hid_sl = lax.all_to_all(hid_split, "grp", split_axis=0, concat_axis=0, tiled=True)
    hid_sl = hid_sl.reshape(slots, f_loc)

    onehot = (ids_all[:, :, None] == jnp.arange(experts, dtype=jnp.int32)).astype(jnp.int32)
    rank = jnp.sum((jnp.cumsum(onehot, axis=1) - onehot) * onehot, axis=2)
    dest = ids_all // exp_dev
    src = jnp.arange(n_grp, dtype=jnp.int32)[:, None]
    target = (((dest * n_grp + src) * exp_dev + ids_all % exp_dev) * most + rank).reshape(slots)
    slot_ids = jnp.arange(slots, dtype=jnp.int32)
    row_slot = jnp.zeros((rows,), jnp.int32).at[target].set(slot_ids)
    gate_buf = jnp.zeros((rows,), jnp.bfloat16).at[target].set(wt_all)
    dy_buf = cot_all[row_slot // top]
    hid_buf = hid_sl[row_slot]

    per_dest = n_grp * exp_dev * most
    dy_recv = lax.all_to_all(dy_buf.reshape(n_exp, per_dest, width), "exp", 0, 0, tiled=True)
    hid_recv = lax.all_to_all(hid_buf.reshape(n_exp, per_dest, f_loc), "exp", 0, 0, tiled=True)
    gate_recv = lax.all_to_all(gate_buf.reshape(n_exp, per_dest), "exp", 0, 0, tiled=True)
    dy_recv = dy_recv.reshape(n_exp, n_grp, exp_dev, most, width)
    hid_recv = hid_recv.reshape(n_exp, n_grp, exp_dev, most, f_loc)
    gate_f = gate_recv.reshape(n_exp, n_grp, exp_dev, most).astype(jnp.float32)

    proj = jnp.einsum("cgjmd,jfd->cgjmf", dy_recv, w_down, preferred_element_type=jnp.float32)
    dh_sl = (gate_f[..., None] * proj).astype(jnp.bfloat16)
    inner_p = jnp.sum(hid_recv.astype(jnp.float32) * proj, axis=4)
    scaled = (gate_f[..., None] * dy_recv.astype(jnp.float32)).astype(jnp.bfloat16)
    parts = jnp.einsum("cgjmf,cgjmd->gjfd", hid_recv, scaled, preferred_element_type=jnp.float32)
    d_weight = jnp.sum((parts * scale).astype(jnp.bfloat16).astype(jnp.float32), axis=0)

    dh_back = lax.all_to_all(dh_sl.reshape(n_exp, per_dest, f_loc), "exp", 0, 0, tiled=True)
    in_back = lax.all_to_all(inner_p.reshape(n_exp, per_dest), "exp", 0, 0, tiled=True)
    dh_slot = dh_back.reshape(rows, f_loc)[target].reshape(n_grp, tok, top, f_loc)
    in_slot = in_back.reshape(rows)[target].reshape(n_grp, tok, top)

    dh_home = lax.all_to_all(dh_slot, "grp", split_axis=0, concat_axis=0, tiled=True)
    d_hidden = jnp.transpose(dh_home, (1, 2, 0, 3)).reshape(tok, top, ffw)
    in_home = lax.all_to_all(in_slot, "grp", split_axis=0, concat_axis=0, tiled=True)
    inner = jnp.sum(in_home, axis=0).astype(jnp.bfloat16)
    d_gate = (inner.astype(jnp.float32) * live[:, None]).astype(jnp.bfloat16)
    return (d_hidden, d_gate, d_weight)


def solution(mesh):
    in_specs = (
        P(("grp", "exp"), None),
        P(("grp", "exp"), None, None),
        P(("grp", "exp"), None),
        P(("grp", "exp"), None),
        P("grp"),
        P("exp", "grp", None),
    )
    out_specs = (P(("grp", "exp"), None, None), P(("grp", "exp"), None), P("exp", "grp", None))
    return jax.shard_map(body, mesh=mesh, in_specs=in_specs, out_specs=out_specs, check_vma=False)
```

```python
import jax
import jax.numpy as jnp
from jax import lax
from jax.sharding import PartitionSpec as P

LOSS_SCALE = 32768


def body(cotangent, hidden, gates, expert_ids, group_counts, w_down):
    tok, top = expert_ids.shape
    ffw = hidden.shape[2]
    width = cotangent.shape[1]
    n_exp = lax.axis_size("exp")
    n_grp = lax.axis_size("grp")
    exp_dev, f_loc = w_down.shape[0], w_down.shape[1]
    experts = exp_dev * n_exp
    most = 5 * tok * top // (4 * experts)
    slots = n_grp * tok * top
    rows = n_exp * n_grp * exp_dev * most
    per_dest = n_grp * exp_dev * most

    count = group_counts[0]
    first_row = lax.axis_index("exp") * tok
    live = (first_row + jnp.arange(tok, dtype=jnp.int32) < count).astype(jnp.float32)
    weighted = (gates.astype(jnp.float32) * live[:, None]).astype(jnp.bfloat16)

    digits = jnp.stack([count // 64, count % 64]).astype(jnp.bfloat16)
    packed = jnp.concatenate(
        [cotangent, expert_ids.astype(jnp.bfloat16), weighted, jnp.broadcast_to(digits, (tok, 2))], axis=1
    )
    got = lax.all_gather(packed, "grp")
    cot_all = got[:, :, :width].reshape(n_grp * tok, width)
    ids_all = got[:, :, width : width + top].astype(jnp.int32).reshape(n_grp, tok * top)
    wt_all = got[:, :, width + top : width + 2 * top].reshape(slots)
    dig = got[:, 0, width + 2 * top :].astype(jnp.float32)
    total = jnp.sum(dig[:, 0] * 64.0 + dig[:, 1])
    scale = LOSS_SCALE / total

    hid_split = jnp.transpose(hidden.reshape(tok, top, n_grp, f_loc), (2, 0, 1, 3))
    hid_sl = lax.all_to_all(hid_split, "grp", split_axis=0, concat_axis=0, tiled=True)
    hid_sl = hid_sl.reshape(slots, f_loc)

    onehot = (ids_all[:, :, None] == jnp.arange(experts, dtype=jnp.int32)).astype(jnp.int32)
    rank = jnp.sum((jnp.cumsum(onehot, axis=1) - onehot) * onehot, axis=2)
    dest = ids_all // exp_dev
    src = jnp.arange(n_grp, dtype=jnp.int32)[:, None]
    target = (((dest * n_grp + src) * exp_dev + ids_all % exp_dev) * most + rank).reshape(slots)
    row_ids = jnp.arange(rows, dtype=jnp.int32)
    pick = (target[None, :] == row_ids[:, None]).astype(jnp.bfloat16)
    pick_tok = jnp.sum(pick.reshape(rows, n_grp * tok, top), axis=2)
    dy_buf = jnp.dot(pick_tok, cot_all, preferred_element_type=jnp.float32).astype(jnp.bfloat16)
    hid_buf = jnp.dot(pick, hid_sl, preferred_element_type=jnp.float32).astype(jnp.bfloat16)
    gate_buf = jnp.dot(pick, wt_all, preferred_element_type=jnp.float32).astype(jnp.bfloat16)

    dy_recv = lax.all_to_all(dy_buf.reshape(n_exp, per_dest, width), "exp", 0, 0, tiled=True)
    hid_recv = lax.all_to_all(hid_buf.reshape(n_exp, per_dest, f_loc), "exp", 0, 0, tiled=True)
    gate_recv = lax.all_to_all(gate_buf.reshape(n_exp, per_dest), "exp", 0, 0, tiled=True)
    dy_recv = dy_recv.reshape(n_exp, n_grp, exp_dev, most, width)
    hid_recv = hid_recv.reshape(n_exp, n_grp, exp_dev, most, f_loc)
    gate_f = gate_recv.reshape(n_exp, n_grp, exp_dev, most).astype(jnp.float32)

    proj = jnp.einsum("cgjmd,jfd->cgjmf", dy_recv, w_down, preferred_element_type=jnp.float32)
    dh_sl = (gate_f[..., None] * proj).astype(jnp.bfloat16)
    inner_p = jnp.sum(hid_recv.astype(jnp.float32) * proj, axis=4)
    scaled = (gate_f[..., None] * dy_recv.astype(jnp.float32)).astype(jnp.bfloat16)
    parts = jnp.einsum("cgjmf,cgjmd->gjfd", hid_recv, scaled, preferred_element_type=jnp.float32)
    d_weight = jnp.sum((parts * scale).astype(jnp.bfloat16).astype(jnp.float32), axis=0)

    dh_back = lax.all_to_all(dh_sl.reshape(n_exp, per_dest, f_loc), "exp", 0, 0, tiled=True)
    in_back = lax.all_to_all(inner_p.reshape(n_exp, per_dest), "exp", 0, 0, tiled=True)
    dh_slot = jnp.dot(pick.T, dh_back.reshape(rows, f_loc), preferred_element_type=jnp.float32)
    dh_slot = dh_slot.astype(jnp.bfloat16).reshape(n_grp, tok, top, f_loc)
    in_slot = jnp.dot(
        in_back.reshape(rows), pick.astype(jnp.float32), precision=lax.Precision.HIGHEST
    ).reshape(n_grp, tok, top)

    dh_home = lax.all_to_all(dh_slot, "grp", split_axis=0, concat_axis=0, tiled=True)
    d_hidden = jnp.transpose(dh_home, (1, 2, 0, 3)).reshape(tok, top, ffw)
    in_home = lax.all_to_all(in_slot, "grp", split_axis=0, concat_axis=0, tiled=True)
    inner = jnp.sum(in_home, axis=0).astype(jnp.bfloat16)
    d_gate = (inner.astype(jnp.float32) * live[:, None]).astype(jnp.bfloat16)
    return (d_hidden, d_gate, d_weight)


def solution(mesh):
    in_specs = (
        P(("grp", "exp"), None),
        P(("grp", "exp"), None, None),
        P(("grp", "exp"), None),
        P(("grp", "exp"), None),
        P("grp"),
        P("exp", "grp", None),
    )
    out_specs = (P(("grp", "exp"), None, None), P(("grp", "exp"), None), P("exp", "grp", None))
    return jax.shard_map(body, mesh=mesh, in_specs=in_specs, out_specs=out_specs, check_vma=False)
```

```python
import jax
import jax.numpy as jnp
from jax import lax
from jax.sharding import PartitionSpec as P

LOSS_SCALE = 32768


def dispatch(ids, wt, cot, hid, experts, exp_dev, most, n_exp):
    n, per = ids.shape
    top = per * n // cot.shape[0]
    rows = n_exp * n * exp_dev * most
    onehot = (ids[:, :, None] == jnp.arange(experts, dtype=jnp.int32)).astype(jnp.int32)
    rank = jnp.sum((jnp.cumsum(onehot, axis=1) - onehot) * onehot, axis=2)
    src = jnp.arange(n, dtype=jnp.int32)[:, None]
    target = ((((ids // exp_dev) * n + src) * exp_dev + ids % exp_dev) * most + rank).reshape(-1)
    pick = (target[None, :] == jnp.arange(rows, dtype=jnp.int32)[:, None]).astype(jnp.bfloat16)
    pick_tok = jnp.sum(pick.reshape(rows, n * per // top, top), axis=2)
    dy_buf = jnp.dot(pick_tok, cot, preferred_element_type=jnp.float32).astype(jnp.bfloat16)
    hid_buf = jnp.dot(pick, hid, preferred_element_type=jnp.float32).astype(jnp.bfloat16)
    gate_buf = jnp.dot(pick, wt, preferred_element_type=jnp.float32).astype(jnp.bfloat16)
    per_dest = n * exp_dev * most
    dy_r = lax.all_to_all(dy_buf.reshape(n_exp, per_dest, -1), "exp", 0, 0, tiled=True)
    hid_r = lax.all_to_all(hid_buf.reshape(n_exp, per_dest, -1), "exp", 0, 0, tiled=True)
    gate_r = lax.all_to_all(gate_buf.reshape(n_exp, per_dest), "exp", 0, 0, tiled=True)
    return target, pick, dy_r, hid_r, gate_r


def expert_work(dy_r, hid_r, gate_r, w_down, scale, n, most):
    n_exp, exp_dev = dy_r.shape[0], w_down.shape[0]
    dy_r = dy_r.reshape(n_exp, n, exp_dev, most, -1)
    hid_r = hid_r.reshape(n_exp, n, exp_dev, most, -1)
    gate_f = gate_r.reshape(n_exp, n, exp_dev, most).astype(jnp.float32)
    proj = jnp.einsum("cgjmd,jfd->cgjmf", dy_r, w_down, preferred_element_type=jnp.float32)
    dh_sl = (gate_f[..., None] * proj).astype(jnp.bfloat16)
    inner_p = jnp.sum(hid_r.astype(jnp.float32) * proj, axis=4)
    scaled = (gate_f[..., None] * dy_r.astype(jnp.float32)).astype(jnp.bfloat16)
    parts = jnp.einsum("cgjmf,cgjmd->gjfd", hid_r, scaled, preferred_element_type=jnp.float32)
    grad = jnp.sum((parts * scale).astype(jnp.bfloat16).astype(jnp.float32), axis=0)
    per_dest = n * exp_dev * most
    dh_b = lax.all_to_all(dh_sl.reshape(n_exp, per_dest, -1), "exp", 0, 0, tiled=True)
    in_b = lax.all_to_all(inner_p.reshape(n_exp, per_dest), "exp", 0, 0, tiled=True)
    return grad, dh_b, in_b


def body(cotangent, hidden, gates, expert_ids, group_counts, w_down):
    tok, top = expert_ids.shape
    ffw = hidden.shape[2]
    width = cotangent.shape[1]
    n_exp = lax.axis_size("exp")
    n_grp = lax.axis_size("grp")
    exp_dev, f_loc = w_down.shape[0], w_down.shape[1]
    experts = exp_dev * n_exp
    most = 5 * tok * top // (4 * experts)
    me = lax.axis_index("grp")

    count = group_counts[0]
    first_row = lax.axis_index("exp") * tok
    live = (first_row + jnp.arange(tok, dtype=jnp.int32) < count).astype(jnp.float32)
    weighted = (gates.astype(jnp.float32) * live[:, None]).astype(jnp.bfloat16)

    digits = jnp.stack([count // 64, count % 64]).astype(jnp.bfloat16)
    packed = jnp.concatenate(
        [cotangent, expert_ids.astype(jnp.bfloat16), weighted, jnp.broadcast_to(digits, (tok, 2))], axis=1
    )
    got = lax.all_gather(packed, "grp")
    dig = got[:, 0, width + 2 * top :].astype(jnp.float32)
    total = jnp.sum(dig[:, 0] * 64.0 + dig[:, 1])
    scale = LOSS_SCALE / total

    hid_split = jnp.transpose(hidden.reshape(tok, top, n_grp, f_loc), (2, 0, 1, 3))
    hid_sl = lax.all_to_all(hid_split, "grp", split_axis=0, concat_axis=0, tiled=True)

    hid_own = jnp.take(hidden.reshape(tok, top, n_grp, f_loc), me, axis=2).reshape(tok * top, f_loc)
    tgt_a, pick_a, dy_a, hid_a, gate_a = dispatch(
        expert_ids.reshape(1, tok * top), weighted.reshape(-1), cotangent, hid_own, experts, exp_dev, most, n_exp
    )
    rel = (me + jnp.arange(1, n_grp, dtype=jnp.int32)) % n_grp
    got_b = jnp.take(got, rel, axis=0)
    n_b = n_grp - 1
    tgt_b, pick_b, dy_b, hid_b, gate_b = dispatch(
        got_b[:, :, width : width + top].astype(jnp.int32).reshape(n_b, tok * top),
        got_b[:, :, width + top : width + 2 * top].reshape(-1),
        got_b[:, :, :width].reshape(n_b * tok, width),
        jnp.take(hid_sl, rel, axis=0).reshape(n_b * tok * top, f_loc),
        experts, exp_dev, most, n_exp,
    )

    grad_a, dh_ba, in_ba = expert_work(dy_a, hid_a, gate_a, w_down, scale, 1, most)
    grad_b, dh_bb, in_bb = expert_work(dy_b, hid_b, gate_b, w_down, scale, n_b, most)
    d_weight = grad_a + grad_b

    dh_rel = jnp.concatenate(
        [
            jnp.dot(pick_a.T, dh_ba.reshape(-1, f_loc), preferred_element_type=jnp.float32),
            jnp.dot(pick_b.T, dh_bb.reshape(-1, f_loc), preferred_element_type=jnp.float32),
        ]
    ).astype(jnp.bfloat16).reshape(n_grp, tok, top, f_loc)
    in_rel = jnp.concatenate([in_ba.reshape(-1)[tgt_a], in_bb.reshape(-1)[tgt_b]]).reshape(n_grp, tok, top)
    back = (jnp.arange(n_grp, dtype=jnp.int32) - me) % n_grp
    dh_slot = jnp.take(dh_rel, back, axis=0)
    in_slot = jnp.take(in_rel, back, axis=0)

    dh_home = lax.all_to_all(dh_slot, "grp", split_axis=0, concat_axis=0, tiled=True)
    d_hidden = jnp.transpose(dh_home, (1, 2, 0, 3)).reshape(tok, top, ffw)
    in_home = lax.all_to_all(in_slot, "grp", split_axis=0, concat_axis=0, tiled=True)
    inner = jnp.sum(in_home, axis=0).astype(jnp.bfloat16)
    d_gate = (inner.astype(jnp.float32) * live[:, None]).astype(jnp.bfloat16)
    return (d_hidden, d_gate, d_weight)


def solution(mesh):
    in_specs = (
        P(("grp", "exp"), None),
        P(("grp", "exp"), None, None),
        P(("grp", "exp"), None),
        P(("grp", "exp"), None),
        P("grp"),
        P("exp", "grp", None),
    )
    out_specs = (P(("grp", "exp"), None, None), P(("grp", "exp"), None), P("exp", "grp", None))
    return jax.shard_map(body, mesh=mesh, in_specs=in_specs, out_specs=out_specs, check_vma=False)
```

```python
import jax
import jax.numpy as jnp
from jax import lax
from jax.sharding import PartitionSpec as P

LOSS_SCALE = 32768


def line_reduce_scatter(parts, n):
    me = lax.axis_index("grp")
    right = jnp.zeros(parts.shape[1:], parts.dtype)
    left = jnp.zeros(parts.shape[1:], parts.dtype)
    for k in range(1, n):
        s_r = jnp.minimum(me + n - k, n - 1)
        s_l = jnp.maximum(me - n + k, 0)
        send_r = (parts[s_r].astype(jnp.float32) + right.astype(jnp.float32)).astype(parts.dtype)
        send_l = (parts[s_l].astype(jnp.float32) + left.astype(jnp.float32)).astype(parts.dtype)
        right = lax.ppermute(send_r, "grp", [(g, g + 1) for g in range(k)])
        left = lax.ppermute(send_l, "grp", [(g, g - 1) for g in range(n - k, n)])
    own = parts[me].astype(jnp.float32)
    return own + right.astype(jnp.float32) + left.astype(jnp.float32)


def body(cotangent, hidden, gates, expert_ids, group_counts, w_down):
    tok = cotangent.shape[0]
    top = expert_ids.shape[1]
    ffw = hidden.shape[2]
    width = cotangent.shape[1]
    n_exp = lax.axis_size("exp")
    n_grp = lax.axis_size("grp")
    exp_dev = w_down.shape[0]
    experts = exp_dev * n_exp
    most = 5 * tok * top // (4 * experts)
    count = group_counts[0]
    first_row = lax.axis_index("exp") * tok
    live = (first_row + jnp.arange(tok, dtype=jnp.int32) < count).astype(jnp.float32)
    total = jnp.sum(lax.all_gather(group_counts, "grp", tiled=True).astype(jnp.float32))
    scale = LOSS_SCALE / total
    weighted = (gates.astype(jnp.float32) * live[:, None]).astype(jnp.bfloat16)
    flat_ids = expert_ids.reshape(-1)
    onehot = (flat_ids[:, None] == jnp.arange(experts, dtype=jnp.int32)[None, :]).astype(jnp.int32)
    rank = jnp.sum((jnp.cumsum(onehot, axis=0) - onehot) * onehot, axis=1)
    target = flat_ids * most + rank
    slot_tok = jnp.arange(tok * top, dtype=jnp.int32) // top
    dy_buf = jnp.zeros((experts * most, width), jnp.bfloat16).at[target].set(cotangent[slot_tok])
    hid_buf = jnp.zeros((experts * most, ffw), jnp.bfloat16).at[target].set(hidden.reshape(-1, ffw))
    gate_buf = jnp.zeros((experts * most,), jnp.bfloat16).at[target].set(weighted.reshape(-1))
    dy_buf = dy_buf.reshape(n_exp, exp_dev * most, width)
    hid_buf = hid_buf.reshape(n_exp, exp_dev * most, ffw)
    gate_buf = gate_buf.reshape(n_exp, exp_dev * most)
    dy_recv, gate_recv = (
        lax.all_to_all(dy_buf, "exp", split_axis=0, concat_axis=0, tiled=True),
        lax.all_to_all(gate_buf, "exp", split_axis=0, concat_axis=0, tiled=True),
    )
    hid_recv = lax.all_to_all(hid_buf, "exp", split_axis=0, concat_axis=0, tiled=True)
    dy_four = dy_recv.reshape(n_exp, exp_dev, most, width)
    hid_four = hid_recv.reshape(n_exp, exp_dev, most, ffw)
    gate_three = gate_recv.reshape(n_exp, exp_dev, most).astype(jnp.float32)
    proj = jnp.einsum(
        "sjmd,jfd->sjmf",
        dy_four,
        lax.all_gather(w_down, "grp", axis=1, tiled=True),
        preferred_element_type=jnp.float32,
    )
    dh_rows = (gate_three[..., None] * proj).astype(jnp.bfloat16)
    inner = jnp.sum(hid_four.astype(jnp.float32) * proj, axis=3).astype(jnp.bfloat16)
    scaled = (gate_three[..., None] * dy_four.astype(jnp.float32)).astype(jnp.bfloat16)
    partial_grad = (
        jnp.einsum(
            "sjmgf,sjmd->gjfd",
            hid_four.reshape(n_exp, exp_dev, most, n_grp, ffw // n_grp),
            scaled,
            preferred_element_type=jnp.float32,
        )
        * scale
    )
    grad_parts = partial_grad.astype(jnp.bfloat16).reshape(n_grp, exp_dev * (ffw // n_grp), width)
    d_weight = line_reduce_scatter(grad_parts, n_grp).reshape(exp_dev, ffw // n_grp, width)
    back_dh, back_inner = (
        lax.all_to_all(
            dh_rows.reshape(n_exp, exp_dev * most, ffw),
            "exp",
            split_axis=0,
            concat_axis=0,
            tiled=True,
        ),
        lax.all_to_all(
            inner.reshape(n_exp, exp_dev * most), "exp", split_axis=0, concat_axis=0, tiled=True
        ),
    )
    d_hidden = back_dh.reshape(experts * most, ffw)[target].reshape(tok, top, ffw)
    inner_tok = back_inner.reshape(-1)[target].reshape(tok, top)
    d_gate = (inner_tok.astype(jnp.float32) * live[:, None]).astype(jnp.bfloat16)
    return (d_hidden, d_gate, d_weight)


def solution(mesh):
    in_specs = (
        P(("grp", "exp"), None),
        P(("grp", "exp"), None, None),
        P(("grp", "exp"), None),
        P(("grp", "exp"), None),
        P("grp"),
        P("exp", "grp", None),
    )
    out_specs = (P(("grp", "exp"), None, None), P(("grp", "exp"), None), P("exp", "grp", None))
    return jax.shard_map(body, mesh=mesh, in_specs=in_specs, out_specs=out_specs, check_vma=False)
```

```python
import jax
import jax.numpy as jnp
from jax import lax
from jax.sharding import PartitionSpec as P

LOSS_SCALE = 32768


def line_all_gather(shard, n):
    me = lax.axis_index("grp")
    from_left, from_right = [], []
    go_r = go_l = shard
    for k in range(1, n):
        go_r = lax.ppermute(go_r, "grp", [(g, g + 1) for g in range(k - 1, n - 1)])
        go_l = lax.ppermute(go_l, "grp", [(g, g - 1) for g in range(1, n - k + 1)])
        from_left.append(go_r)
        from_right.append(go_l)
    pieces = jnp.stack(from_left[::-1] + [shard] + from_right)
    return lax.dynamic_slice_in_dim(pieces, n - 1 - me, n, axis=0)


def line_reduce_scatter(parts, n):
    me = lax.axis_index("grp")
    right = jnp.zeros(parts.shape[1:], parts.dtype)
    left = jnp.zeros(parts.shape[1:], parts.dtype)
    for k in range(1, n):
        s_r = jnp.minimum(me + n - k, n - 1)
        s_l = jnp.maximum(me - n + k, 0)
        send_r = (parts[s_r].astype(jnp.float32) + right.astype(jnp.float32)).astype(parts.dtype)
        send_l = (parts[s_l].astype(jnp.float32) + left.astype(jnp.float32)).astype(parts.dtype)
        right = lax.ppermute(send_r, "grp", [(g, g + 1) for g in range(k)])
        left = lax.ppermute(send_l, "grp", [(g, g - 1) for g in range(n - k, n)])
    own = parts[me].astype(jnp.float32)
    return own + right.astype(jnp.float32) + left.astype(jnp.float32)


def body(cotangent, hidden, gates, expert_ids, group_counts, w_down):
    tok = cotangent.shape[0]
    top = expert_ids.shape[1]
    ffw = hidden.shape[2]
    width = cotangent.shape[1]
    n_exp = lax.axis_size("exp")
    n_grp = lax.axis_size("grp")
    exp_dev = w_down.shape[0]
    experts = exp_dev * n_exp
    most = 5 * tok * top // (4 * experts)
    count = group_counts[0]
    first_row = lax.axis_index("exp") * tok
    live = (first_row + jnp.arange(tok, dtype=jnp.int32) < count).astype(jnp.float32)
    total = jnp.sum(lax.all_gather(group_counts, "grp", tiled=True).astype(jnp.float32))
    scale = LOSS_SCALE / total
    weighted = (gates.astype(jnp.float32) * live[:, None]).astype(jnp.bfloat16)
    flat_ids = expert_ids.reshape(-1)
    onehot = (flat_ids[:, None] == jnp.arange(experts, dtype=jnp.int32)[None, :]).astype(jnp.int32)
    rank = jnp.sum((jnp.cumsum(onehot, axis=0) - onehot) * onehot, axis=1)
    target = flat_ids * most + rank
    slot_tok = jnp.arange(tok * top, dtype=jnp.int32) // top
    dy_buf = jnp.zeros((experts * most, width), jnp.bfloat16).at[target].set(cotangent[slot_tok])
    hid_buf = jnp.zeros((experts * most, ffw), jnp.bfloat16).at[target].set(hidden.reshape(-1, ffw))
    gate_buf = jnp.zeros((experts * most,), jnp.bfloat16).at[target].set(weighted.reshape(-1))
    dy_buf = dy_buf.reshape(n_exp, exp_dev * most, width)
    hid_buf = hid_buf.reshape(n_exp, exp_dev * most, ffw)
    gate_buf = gate_buf.reshape(n_exp, exp_dev * most)
    dy_recv, gate_recv = (
        lax.all_to_all(dy_buf, "exp", split_axis=0, concat_axis=0, tiled=True),
        lax.all_to_all(gate_buf, "exp", split_axis=0, concat_axis=0, tiled=True),
    )
    hid_recv = lax.all_to_all(hid_buf, "exp", split_axis=0, concat_axis=0, tiled=True)
    dy_four = dy_recv.reshape(n_exp, exp_dev, most, width)
    hid_four = hid_recv.reshape(n_exp, exp_dev, most, ffw)
    gate_three = gate_recv.reshape(n_exp, exp_dev, most).astype(jnp.float32)
    proj = jnp.einsum(
        "sjmd,jfd->sjmf",
        dy_four,
        jnp.transpose(line_all_gather(w_down, n_grp), (1, 0, 2, 3)).reshape(exp_dev, ffw, width),
        preferred_element_type=jnp.float32,
    )
    dh_rows = (gate_three[..., None] * proj).astype(jnp.bfloat16)
    inner = jnp.sum(hid_four.astype(jnp.float32) * proj, axis=3).astype(jnp.bfloat16)
    scaled = (gate_three[..., None] * dy_four.astype(jnp.float32)).astype(jnp.bfloat16)
    partial_grad = (
        jnp.einsum(
            "sjmgf,sjmd->gjfd",
            hid_four.reshape(n_exp, exp_dev, most, n_grp, ffw // n_grp),
            scaled,
            preferred_element_type=jnp.float32,
        )
        * scale
    )
    grad_parts = partial_grad.astype(jnp.bfloat16).reshape(n_grp, exp_dev * (ffw // n_grp), width)
    d_weight = line_reduce_scatter(grad_parts, n_grp).reshape(exp_dev, ffw // n_grp, width)
    back_dh, back_inner = (
        lax.all_to_all(
            dh_rows.reshape(n_exp, exp_dev * most, ffw),
            "exp",
            split_axis=0,
            concat_axis=0,
            tiled=True,
        ),
        lax.all_to_all(
            inner.reshape(n_exp, exp_dev * most), "exp", split_axis=0, concat_axis=0, tiled=True
        ),
    )
    d_hidden = back_dh.reshape(experts * most, ffw)[target].reshape(tok, top, ffw)
    inner_tok = back_inner.reshape(-1)[target].reshape(tok, top)
    d_gate = (inner_tok.astype(jnp.float32) * live[:, None]).astype(jnp.bfloat16)
    return (d_hidden, d_gate, d_weight)


def solution(mesh):
    in_specs = (
        P(("grp", "exp"), None),
        P(("grp", "exp"), None, None),
        P(("grp", "exp"), None),
        P(("grp", "exp"), None),
        P("grp"),
        P("exp", "grp", None),
    )
    out_specs = (P(("grp", "exp"), None, None), P(("grp", "exp"), None), P("exp", "grp", None))
    return jax.shard_map(body, mesh=mesh, in_specs=in_specs, out_specs=out_specs, check_vma=False)
```

```python
import jax
import jax.numpy as jnp
from jax import lax
from jax.sharding import PartitionSpec as P

LOSS_SCALE = 32768


def line_all_gather(shard, n, gate):
    me = lax.axis_index("grp")
    first = jnp.where(gate, shard, jnp.zeros_like(shard))
    from_left, from_right = [], []
    go_r = go_l = first
    for k in range(1, n):
        go_r = lax.ppermute(go_r, "grp", [(g, g + 1) for g in range(k - 1, n - 1)])
        go_l = lax.ppermute(go_l, "grp", [(g, g - 1) for g in range(1, n - k + 1)])
        from_left.append(go_r)
        from_right.append(go_l)
    full = jnp.zeros(shard.shape[:1] + (n,) + shard.shape[1:], shard.dtype)
    for k in range(n - 1, 0, -1):
        full = lax.dynamic_update_index_in_dim(full, from_left[k - 1], jnp.maximum(me - k, 0), 1)
    for k in range(n - 1, 0, -1):
        full = lax.dynamic_update_index_in_dim(full, from_right[k - 1], jnp.minimum(me + k, n - 1), 1)
    return lax.dynamic_update_index_in_dim(full, shard, me, 1)


def line_reduce_scatter(parts, n):
    me = lax.axis_index("grp")
    right = jnp.zeros(parts.shape[1:], parts.dtype)
    left = jnp.zeros(parts.shape[1:], parts.dtype)
    for k in range(1, n):
        s_r = jnp.minimum(me + n - k, n - 1)
        s_l = jnp.maximum(me - n + k, 0)
        send_r = (parts[s_r].astype(jnp.float32) + right.astype(jnp.float32)).astype(parts.dtype)
        send_l = (parts[s_l].astype(jnp.float32) + left.astype(jnp.float32)).astype(parts.dtype)
        right = lax.ppermute(send_r, "grp", [(g, g + 1) for g in range(k)])
        left = lax.ppermute(send_l, "grp", [(g, g - 1) for g in range(n - k, n)])
    own = parts[me].astype(jnp.float32)
    return own + right.astype(jnp.float32) + left.astype(jnp.float32)


def body(cotangent, hidden, gates, expert_ids, group_counts, w_down):
    tok = cotangent.shape[0]
    top = expert_ids.shape[1]
    ffw = hidden.shape[2]
    width = cotangent.shape[1]
    n_exp = lax.axis_size("exp")
    n_grp = lax.axis_size("grp")
    exp_dev = w_down.shape[0]
    experts = exp_dev * n_exp
    most = 5 * tok * top // (4 * experts)
    count = group_counts[0]
    first_row = lax.axis_index("exp") * tok
    live = (first_row + jnp.arange(tok, dtype=jnp.int32) < count).astype(jnp.float32)
    total = jnp.sum(lax.all_gather(group_counts, "grp", tiled=True).astype(jnp.float32))
    scale = LOSS_SCALE / total
    weighted = (gates.astype(jnp.float32) * live[:, None]).astype(jnp.bfloat16)
    flat_ids = expert_ids.reshape(-1)
    onehot = (flat_ids[:, None] == jnp.arange(experts, dtype=jnp.int32)[None, :]).astype(jnp.int32)
    rank = jnp.sum((jnp.cumsum(onehot, axis=0) - onehot) * onehot, axis=1)
    target = flat_ids * most + rank
    slot_tok = jnp.arange(tok * top, dtype=jnp.int32) // top
    dy_buf = jnp.zeros((experts * most, width), jnp.bfloat16).at[target].set(cotangent[slot_tok])
    hid_buf = jnp.zeros((experts * most, ffw), jnp.bfloat16).at[target].set(hidden.reshape(-1, ffw))
    gate_buf = jnp.zeros((experts * most,), jnp.bfloat16).at[target].set(weighted.reshape(-1))
    dy_buf = dy_buf.reshape(n_exp, exp_dev * most, width)
    hid_buf = hid_buf.reshape(n_exp, exp_dev * most, ffw)
    gate_buf = gate_buf.reshape(n_exp, exp_dev * most)
    dy_recv, gate_recv = (
        lax.all_to_all(dy_buf, "exp", split_axis=0, concat_axis=0, tiled=True),
        lax.all_to_all(gate_buf, "exp", split_axis=0, concat_axis=0, tiled=True),
    )
    hid_recv = lax.all_to_all(hid_buf, "exp", split_axis=0, concat_axis=0, tiled=True)
    dy_four = dy_recv.reshape(n_exp, exp_dev, most, width)
    hid_four = hid_recv.reshape(n_exp, exp_dev, most, ffw)
    gate_three = gate_recv.reshape(n_exp, exp_dev, most).astype(jnp.float32)
    proj = jnp.einsum(
        "sjmd,jfd->sjmf",
        dy_four,
        line_all_gather(w_down, n_grp, total > 0).reshape(exp_dev, ffw, width),
        preferred_element_type=jnp.float32,
    )
    dh_rows = (gate_three[..., None] * proj).astype(jnp.bfloat16)
    inner = jnp.sum(hid_four.astype(jnp.float32) * proj, axis=3).astype(jnp.bfloat16)
    scaled = (gate_three[..., None] * dy_four.astype(jnp.float32)).astype(jnp.bfloat16)
    partial_grad = (
        jnp.einsum(
            "sjmgf,sjmd->gjfd",
            hid_four.reshape(n_exp, exp_dev, most, n_grp, ffw // n_grp),
            scaled,
            preferred_element_type=jnp.float32,
        )
        * scale
    )
    grad_parts = partial_grad.astype(jnp.bfloat16).reshape(n_grp, exp_dev * (ffw // n_grp), width)
    d_weight = line_reduce_scatter(grad_parts, n_grp).reshape(exp_dev, ffw // n_grp, width)
    back_dh, back_inner = (
        lax.all_to_all(
            dh_rows.reshape(n_exp, exp_dev * most, ffw),
            "exp",
            split_axis=0,
            concat_axis=0,
            tiled=True,
        ),
        lax.all_to_all(
            inner.reshape(n_exp, exp_dev * most), "exp", split_axis=0, concat_axis=0, tiled=True
        ),
    )
    d_hidden = back_dh.reshape(experts * most, ffw)[target].reshape(tok, top, ffw)
    inner_tok = back_inner.reshape(-1)[target].reshape(tok, top)
    d_gate = (inner_tok.astype(jnp.float32) * live[:, None]).astype(jnp.bfloat16)
    return (d_hidden, d_gate, d_weight)


def solution(mesh):
    in_specs = (
        P(("grp", "exp"), None),
        P(("grp", "exp"), None, None),
        P(("grp", "exp"), None),
        P(("grp", "exp"), None),
        P("grp"),
        P("exp", "grp", None),
    )
    out_specs = (P(("grp", "exp"), None, None), P(("grp", "exp"), None), P("exp", "grp", None))
    return jax.shard_map(body, mesh=mesh, in_specs=in_specs, out_specs=out_specs, check_vma=False)
```

```python
import jax
import jax.numpy as jnp
from jax import lax
from jax.sharding import PartitionSpec as P

LOSS_SCALE = 32768


def line_reduce_scatter(parts, n):
    me = lax.axis_index("grp")
    right = jnp.zeros(parts.shape[1:], parts.dtype)
    left = jnp.zeros(parts.shape[1:], parts.dtype)
    for k in range(1, n):
        s_r = jnp.minimum(me + n - k, n - 1)
        s_l = jnp.maximum(me - n + k, 0)
        send_r = (parts[s_r].astype(jnp.float32) + right.astype(jnp.float32)).astype(parts.dtype)
        send_l = (parts[s_l].astype(jnp.float32) + left.astype(jnp.float32)).astype(parts.dtype)
        right = lax.ppermute(send_r, "grp", [(g, g + 1) for g in range(k)])
        left = lax.ppermute(send_l, "grp", [(g, g - 1) for g in range(n - k, n)])
    own = parts[me].astype(jnp.float32)
    return own + right.astype(jnp.float32) + left.astype(jnp.float32)


def body(cotangent, hidden, gates, expert_ids, group_counts, w_down):
    tok = cotangent.shape[0]
    top = expert_ids.shape[1]
    ffw = hidden.shape[2]
    width = cotangent.shape[1]
    n_exp = lax.axis_size("exp")
    n_grp = lax.axis_size("grp")
    exp_dev = w_down.shape[0]
    experts = exp_dev * n_exp
    most = 5 * tok * top // (4 * experts)
    count = group_counts[0]
    first_row = lax.axis_index("exp") * tok
    live = (first_row + jnp.arange(tok, dtype=jnp.int32) < count).astype(jnp.float32)
    total = jnp.sum(lax.all_gather(group_counts, "grp", tiled=True).astype(jnp.float32))
    scale = LOSS_SCALE / total
    weighted = (gates.astype(jnp.float32) * live[:, None]).astype(jnp.bfloat16)
    flat_ids = expert_ids.reshape(-1)
    onehot = (flat_ids[:, None] == jnp.arange(experts, dtype=jnp.int32)[None, :]).astype(jnp.int32)
    rank = jnp.sum((jnp.cumsum(onehot, axis=0) - onehot) * onehot, axis=1)
    target = flat_ids * most + rank
    slot_tok = jnp.arange(tok * top, dtype=jnp.int32) // top
    dy_buf = jnp.zeros((experts * most, width), jnp.bfloat16).at[target].set(cotangent[slot_tok])
    hid_buf = jnp.zeros((experts * most, ffw), jnp.bfloat16).at[target].set(hidden.reshape(-1, ffw))
    gate_buf = jnp.zeros((experts * most,), jnp.bfloat16).at[target].set(weighted.reshape(-1))
    dy_buf = dy_buf.reshape(n_exp, exp_dev * most, width)
    hid_buf = hid_buf.reshape(n_exp, exp_dev * most, ffw)
    gate_buf = gate_buf.reshape(n_exp, exp_dev * most)
    dy_recv, gate_recv = (
        lax.all_to_all(dy_buf, "exp", split_axis=0, concat_axis=0, tiled=True),
        lax.all_to_all(gate_buf, "exp", split_axis=0, concat_axis=0, tiled=True),
    )
    hid_recv = lax.all_to_all(hid_buf, "exp", split_axis=0, concat_axis=0, tiled=True)
    dy_four = dy_recv.reshape(n_exp, exp_dev, most, width)
    hid_four = hid_recv.reshape(n_exp, exp_dev, most, ffw)
    gate_three = gate_recv.reshape(n_exp, exp_dev, most).astype(jnp.float32)
    w_full = lax.all_gather(w_down, "grp", axis=1, tiled=True)
    proj = jnp.einsum("sjmd,jfd->sjmf", dy_four, w_full, preferred_element_type=jnp.float32)
    after_gather = jnp.abs(w_full[0, 0, 0]) < jnp.inf
    dh_rows = (gate_three[..., None] * proj).astype(jnp.bfloat16)
    inner = jnp.sum(hid_four.astype(jnp.float32) * proj, axis=3).astype(jnp.bfloat16)
    scaled = (gate_three[..., None] * dy_four.astype(jnp.float32)).astype(jnp.bfloat16)
    partial_grad = (
        jnp.einsum(
            "sjmgf,sjmd->gjfd",
            hid_four.reshape(n_exp, exp_dev, most, n_grp, ffw // n_grp),
            scaled,
            preferred_element_type=jnp.float32,
        )
        * scale
    )
    grad_parts = jnp.where(after_gather, partial_grad, 0.0).astype(jnp.bfloat16)
    grad_parts = grad_parts.reshape(n_grp, exp_dev * (ffw // n_grp), width)
    d_weight = line_reduce_scatter(grad_parts, n_grp).reshape(exp_dev, ffw // n_grp, width)
    back_dh, back_inner = (
        lax.all_to_all(
            dh_rows.reshape(n_exp, exp_dev * most, ffw),
            "exp",
            split_axis=0,
            concat_axis=0,
            tiled=True,
        ),
        lax.all_to_all(
            inner.reshape(n_exp, exp_dev * most), "exp", split_axis=0, concat_axis=0, tiled=True
        ),
    )
    d_hidden = back_dh.reshape(experts * most, ffw)[target].reshape(tok, top, ffw)
    inner_tok = back_inner.reshape(-1)[target].reshape(tok, top)
    d_gate = (inner_tok.astype(jnp.float32) * live[:, None]).astype(jnp.bfloat16)
    return (d_hidden, d_gate, d_weight)


def solution(mesh):
    in_specs = (
        P(("grp", "exp"), None),
        P(("grp", "exp"), None, None),
        P(("grp", "exp"), None),
        P(("grp", "exp"), None),
        P("grp"),
        P("exp", "grp", None),
    )
    out_specs = (P(("grp", "exp"), None, None), P(("grp", "exp"), None), P("exp", "grp", None))
    return jax.shard_map(body, mesh=mesh, in_specs=in_specs, out_specs=out_specs, check_vma=False)
```

```python
import jax
import jax.numpy as jnp
from jax import lax
from jax.sharding import PartitionSpec as P

LOSS_SCALE = 32768


def line_all_gather(shard, n, gate):
    me = lax.axis_index("grp")
    first = jnp.where(gate, shard, jnp.zeros_like(shard))
    from_left, from_right = [], []
    go_r = go_l = first
    for k in range(1, n):
        go_r = lax.ppermute(go_r, "grp", [(g, g + 1) for g in range(k - 1, n - 1)])
        go_l = lax.ppermute(go_l, "grp", [(g, g - 1) for g in range(1, n - k + 1)])
        from_left.append(go_r)
        from_right.append(go_l)
    full = jnp.zeros(shard.shape[:1] + (n,) + shard.shape[1:], shard.dtype)
    for k in range(n - 1, 0, -1):
        full = lax.dynamic_update_index_in_dim(full, from_left[k - 1], jnp.maximum(me - k, 0), 1)
    for k in range(n - 1, 0, -1):
        full = lax.dynamic_update_index_in_dim(full, from_right[k - 1], jnp.minimum(me + k, n - 1), 1)
    return lax.dynamic_update_index_in_dim(full, shard, me, 1)


def line_reduce_scatter(parts, n):
    me = lax.axis_index("grp")
    right = jnp.zeros(parts.shape[1:], parts.dtype)
    left = jnp.zeros(parts.shape[1:], parts.dtype)
    for k in range(1, n):
        s_r = jnp.minimum(me + n - k, n - 1)
        s_l = jnp.maximum(me - n + k, 0)
        send_r = (parts[s_r].astype(jnp.float32) + right.astype(jnp.float32)).astype(parts.dtype)
        send_l = (parts[s_l].astype(jnp.float32) + left.astype(jnp.float32)).astype(parts.dtype)
        right = lax.ppermute(send_r, "grp", [(g, g + 1) for g in range(k)])
        left = lax.ppermute(send_l, "grp", [(g, g - 1) for g in range(n - k, n)])
    own = parts[me].astype(jnp.float32)
    return own + right.astype(jnp.float32) + left.astype(jnp.float32)


def body(cotangent, hidden, gates, expert_ids, group_counts, w_down):
    tok = cotangent.shape[0]
    top = expert_ids.shape[1]
    ffw = hidden.shape[2]
    width = cotangent.shape[1]
    n_exp = lax.axis_size("exp")
    n_grp = lax.axis_size("grp")
    exp_dev = w_down.shape[0]
    experts = exp_dev * n_exp
    most = 5 * tok * top // (4 * experts)
    count = group_counts[0]
    first_row = lax.axis_index("exp") * tok
    live = (first_row + jnp.arange(tok, dtype=jnp.int32) < count).astype(jnp.float32)
    total = jnp.sum(lax.all_gather(group_counts, "grp", tiled=True).astype(jnp.float32))
    scale = LOSS_SCALE / total
    weighted = (gates.astype(jnp.float32) * live[:, None]).astype(jnp.bfloat16)
    flat_ids = expert_ids.reshape(-1)
    onehot = (flat_ids[:, None] == jnp.arange(experts, dtype=jnp.int32)[None, :]).astype(jnp.int32)
    rank = jnp.sum((jnp.cumsum(onehot, axis=0) - onehot) * onehot, axis=1)
    target = flat_ids * most + rank
    slot_tok = jnp.arange(tok * top, dtype=jnp.int32) // top
    dy_buf = jnp.zeros((experts * most, width), jnp.bfloat16).at[target].set(cotangent[slot_tok])
    hid_buf = jnp.zeros((experts * most, ffw), jnp.bfloat16).at[target].set(hidden.reshape(-1, ffw))
    gate_buf = jnp.zeros((experts * most,), jnp.bfloat16).at[target].set(weighted.reshape(-1))
    dy_buf = dy_buf.reshape(n_exp, exp_dev * most, width)
    hid_buf = hid_buf.reshape(n_exp, exp_dev * most, ffw)
    gate_buf = gate_buf.reshape(n_exp, exp_dev * most)
    dy_recv, gate_recv = (
        lax.all_to_all(dy_buf, "exp", split_axis=0, concat_axis=0, tiled=True),
        lax.all_to_all(gate_buf, "exp", split_axis=0, concat_axis=0, tiled=True),
    )
    hid_recv = lax.all_to_all(hid_buf, "exp", split_axis=0, concat_axis=0, tiled=True)
    dy_four = dy_recv.reshape(n_exp, exp_dev, most, width)
    hid_four = hid_recv.reshape(n_exp, exp_dev, most, ffw)
    gate_three = gate_recv.reshape(n_exp, exp_dev, most).astype(jnp.float32)
    proj = jnp.einsum(
        "sjmd,jfd->sjmf",
        dy_four,
        jnp.concatenate(
            [line_all_gather(w_down[j : j + 1], n_grp, total > 0) for j in range(exp_dev)]
        ).reshape(exp_dev, ffw, width),
        preferred_element_type=jnp.float32,
    )
    dh_rows = (gate_three[..., None] * proj).astype(jnp.bfloat16)
    inner = jnp.sum(hid_four.astype(jnp.float32) * proj, axis=3).astype(jnp.bfloat16)
    scaled = (gate_three[..., None] * dy_four.astype(jnp.float32)).astype(jnp.bfloat16)
    partial_grad = (
        jnp.einsum(
            "sjmgf,sjmd->jgfd",
            hid_four.reshape(n_exp, exp_dev, most, n_grp, ffw // n_grp),
            scaled,
            preferred_element_type=jnp.float32,
        )
        * scale
    )
    grad_parts = partial_grad.astype(jnp.bfloat16)
    d_weight = jnp.stack([line_reduce_scatter(grad_parts[j], n_grp) for j in range(exp_dev)])
    back_dh, back_inner = (
        lax.all_to_all(
            dh_rows.reshape(n_exp, exp_dev * most, ffw),
            "exp",
            split_axis=0,
            concat_axis=0,
            tiled=True,
        ),
        lax.all_to_all(
            inner.reshape(n_exp, exp_dev * most), "exp", split_axis=0, concat_axis=0, tiled=True
        ),
    )
    d_hidden = back_dh.reshape(experts * most, ffw)[target].reshape(tok, top, ffw)
    inner_tok = back_inner.reshape(-1)[target].reshape(tok, top)
    d_gate = (inner_tok.astype(jnp.float32) * live[:, None]).astype(jnp.bfloat16)
    return (d_hidden, d_gate, d_weight)


def solution(mesh):
    in_specs = (
        P(("grp", "exp"), None),
        P(("grp", "exp"), None, None),
        P(("grp", "exp"), None),
        P(("grp", "exp"), None),
        P("grp"),
        P("exp", "grp", None),
    )
    out_specs = (P(("grp", "exp"), None, None), P(("grp", "exp"), None), P("exp", "grp", None))
    return jax.shard_map(body, mesh=mesh, in_specs=in_specs, out_specs=out_specs, check_vma=False)
```

```python
import jax
import jax.numpy as jnp
from jax import lax
from jax.sharding import PartitionSpec as P

LOSS_SCALE = 32768


def dispatch(ids, wt, cot, hid, experts, exp_dev, most, n_exp):
    n, per = ids.shape
    top = per * n // cot.shape[0]
    rows = n_exp * n * exp_dev * most
    onehot = (ids[:, :, None] == jnp.arange(experts, dtype=jnp.int32)).astype(jnp.int32)
    rank = jnp.sum((jnp.cumsum(onehot, axis=1) - onehot) * onehot, axis=2)
    src = jnp.arange(n, dtype=jnp.int32)[:, None]
    target = ((((ids // exp_dev) * n + src) * exp_dev + ids % exp_dev) * most + rank).reshape(-1)
    pick = (target[None, :] == jnp.arange(rows, dtype=jnp.int32)[:, None]).astype(jnp.bfloat16)
    pick_tok = jnp.sum(pick.reshape(rows, n * per // top, top), axis=2)
    per_dest = n * exp_dev * most
    dy_buf = jnp.dot(pick_tok, cot, preferred_element_type=jnp.float32).astype(jnp.bfloat16)
    gate_buf = jnp.dot(pick, wt, preferred_element_type=jnp.float32).astype(jnp.bfloat16)
    dy_r = lax.all_to_all(dy_buf.reshape(n_exp, per_dest, -1), "exp", 0, 0, tiled=True)
    gate_r = lax.all_to_all(gate_buf.reshape(n_exp, per_dest), "exp", 0, 0, tiled=True)
    hid_r = None
    if hid is not None:
        hid_buf = jnp.dot(pick, hid, preferred_element_type=jnp.float32).astype(jnp.bfloat16)
        hid_r = lax.all_to_all(hid_buf.reshape(n_exp, per_dest, -1), "exp", 0, 0, tiled=True)
    return pick, dy_r, gate_r, hid_r


def proj_home(pick, dy_r, w_down, n, most):
    n_exp, exp_dev = dy_r.shape[0], w_down.shape[0]
    dy_r = dy_r.reshape(n_exp, n, exp_dev, most, -1)
    proj = jnp.einsum("cgjmd,jfd->cgjmf", dy_r, w_down, preferred_element_type=jnp.float32)
    back = lax.all_to_all(
        proj.astype(jnp.bfloat16).reshape(n_exp, n * exp_dev * most, -1), "exp", 0, 0, tiled=True
    )
    return jnp.dot(pick.T, back.reshape(-1, back.shape[-1]), preferred_element_type=jnp.float32)


def body(cotangent, hidden, gates, expert_ids, group_counts, w_down):
    tok, top = expert_ids.shape
    ffw = hidden.shape[2]
    width = cotangent.shape[1]
    n_exp = lax.axis_size("exp")
    n_grp = lax.axis_size("grp")
    exp_dev, f_loc = w_down.shape[0], w_down.shape[1]
    experts = exp_dev * n_exp
    most = 5 * tok * top // (4 * experts)
    me = lax.axis_index("grp")

    count = group_counts[0]
    first_row = lax.axis_index("exp") * tok
    live = (first_row + jnp.arange(tok, dtype=jnp.int32) < count).astype(jnp.float32)
    weighted = (gates.astype(jnp.float32) * live[:, None]).astype(jnp.bfloat16)

    digits = jnp.stack([count // 64, count % 64]).astype(jnp.bfloat16)
    packed = jnp.concatenate(
        [cotangent, expert_ids.astype(jnp.bfloat16), weighted, jnp.broadcast_to(digits, (tok, 2))], axis=1
    )
    got = lax.all_gather(packed, "grp")
    dig = got[:, 0, width + 2 * top :].astype(jnp.float32)
    total = jnp.sum(dig[:, 0] * 64.0 + dig[:, 1])
    scale = LOSS_SCALE / total

    pick_a, dy_a, gate_a, hid_a = dispatch(
        expert_ids.reshape(1, tok * top), weighted.reshape(-1), cotangent,
        hidden.reshape(tok * top, ffw), experts, exp_dev, most, n_exp,
    )
    gate_fa = gate_a.reshape(n_exp, exp_dev, most).astype(jnp.float32)
    dy_fa = dy_a.reshape(n_exp, exp_dev, most, width)
    scaled = (gate_fa[..., None] * dy_fa.astype(jnp.float32)).astype(jnp.bfloat16)
    partial_grad = (
        jnp.einsum(
            "sjmgf,sjmd->gjfd",
            hid_a.reshape(n_exp, exp_dev, most, n_grp, f_loc),
            scaled,
            preferred_element_type=jnp.float32,
        )
        * scale
    )
    grad_rows = partial_grad.astype(jnp.bfloat16).reshape(n_grp * exp_dev * f_loc, width)
    d_weight = (
        lax.psum_scatter(grad_rows, "grp", scatter_dimension=0, tiled=True)
        .reshape(exp_dev, f_loc, width)
        .astype(jnp.float32)
    )

    rel = (me + jnp.arange(1, n_grp, dtype=jnp.int32)) % n_grp
    got_b = jnp.take(got, rel, axis=0)
    n_b = n_grp - 1
    pick_b, dy_b, _, _ = dispatch(
        got_b[:, :, width : width + top].astype(jnp.int32).reshape(n_b, tok * top),
        got_b[:, :, width + top : width + 2 * top].reshape(-1),
        got_b[:, :, :width].reshape(n_b * tok, width),
        None, experts, exp_dev, most, n_exp,
    )

    proj_rel = jnp.concatenate(
        [proj_home(pick_a, dy_a, w_down, 1, most), proj_home(pick_b, dy_b, w_down, n_b, most)]
    ).astype(jnp.bfloat16).reshape(n_grp, tok, top, f_loc)
    back = (jnp.arange(n_grp, dtype=jnp.int32) - me) % n_grp
    proj_slot = jnp.take(proj_rel, back, axis=0)
    proj_got = lax.all_to_all(proj_slot, "grp", split_axis=0, concat_axis=0, tiled=True)
    proj = jnp.transpose(proj_got, (1, 2, 0, 3)).reshape(tok, top, ffw).astype(jnp.float32)

    d_hidden = (weighted.astype(jnp.float32)[..., None] * proj).astype(jnp.bfloat16)
    inner = jnp.sum(hidden.astype(jnp.float32) * proj, axis=2).astype(jnp.bfloat16)
    d_gate = (inner.astype(jnp.float32) * live[:, None]).astype(jnp.bfloat16)
    return (d_hidden, d_gate, d_weight)


def solution(mesh):
    in_specs = (
        P(("grp", "exp"), None),
        P(("grp", "exp"), None, None),
        P(("grp", "exp"), None),
        P(("grp", "exp"), None),
        P("grp"),
        P("exp", "grp", None),
    )
    out_specs = (P(("grp", "exp"), None, None), P(("grp", "exp"), None), P("exp", "grp", None))
    return jax.shard_map(body, mesh=mesh, in_specs=in_specs, out_specs=out_specs, check_vma=False)
```

```python
import jax
import jax.numpy as jnp
from jax import lax
from jax.sharding import PartitionSpec as P

LOSS_SCALE = 32768


def rank_of(ids, experts):
    onehot = (ids[:, :, None] == jnp.arange(experts, dtype=jnp.int32)).astype(jnp.int32)
    return jnp.sum((jnp.cumsum(onehot, axis=1) - onehot) * onehot, axis=2)


def dispatch(ids, rank, wt, cot, hid, exp_dev, most, n_exp):
    n, per = ids.shape
    top = per * n // cot.shape[0]
    rows = n_exp * n * exp_dev * most
    src = jnp.arange(n, dtype=jnp.int32)[:, None]
    target = ((((ids // exp_dev) * n + src) * exp_dev + ids % exp_dev) * most + rank).reshape(-1)
    pick = (target[None, :] == jnp.arange(rows, dtype=jnp.int32)[:, None]).astype(jnp.bfloat16)
    pick_tok = jnp.sum(pick.reshape(rows, n * per // top, top), axis=2)
    per_dest = n * exp_dev * most
    dy_buf = jnp.dot(pick_tok, cot, preferred_element_type=jnp.float32).astype(jnp.bfloat16)
    gate_buf = jnp.dot(pick, wt, preferred_element_type=jnp.float32).astype(jnp.bfloat16)
    dy_r = lax.all_to_all(dy_buf.reshape(n_exp, per_dest, -1), "exp", 0, 0, tiled=True)
    gate_r = lax.all_to_all(gate_buf.reshape(n_exp, per_dest), "exp", 0, 0, tiled=True)
    hid_r = None
    if hid is not None:
        hid_buf = jnp.dot(pick, hid, preferred_element_type=jnp.float32).astype(jnp.bfloat16)
        hid_r = lax.all_to_all(hid_buf.reshape(n_exp, per_dest, -1), "exp", 0, 0, tiled=True)
    return pick, dy_r, gate_r, hid_r


def proj_home(pick, dy_r, w_down, n, most):
    n_exp, exp_dev = dy_r.shape[0], w_down.shape[0]
    dy_r = dy_r.reshape(n_exp, n, exp_dev, most, -1)
    proj = jnp.einsum("cgjmd,jfd->cgjmf", dy_r, w_down, preferred_element_type=jnp.float32)
    back = lax.all_to_all(
        proj.astype(jnp.bfloat16).reshape(n_exp, n * exp_dev * most, -1), "exp", 0, 0, tiled=True
    )
    return jnp.dot(pick.T, back.reshape(-1, back.shape[-1]), preferred_element_type=jnp.float32)


def body(cotangent, hidden, gates, expert_ids, group_counts, w_down):
    tok, top = expert_ids.shape
    ffw = hidden.shape[2]
    width = cotangent.shape[1]
    n_exp = lax.axis_size("exp")
    n_grp = lax.axis_size("grp")
    exp_dev, f_loc = w_down.shape[0], w_down.shape[1]
    experts = exp_dev * n_exp
    most = 5 * tok * top // (4 * experts)
    me = lax.axis_index("grp")

    count = group_counts[0]
    first_row = lax.axis_index("exp") * tok
    live = (first_row + jnp.arange(tok, dtype=jnp.int32) < count).astype(jnp.float32)
    weighted = (gates.astype(jnp.float32) * live[:, None]).astype(jnp.bfloat16)

    rank_own = rank_of(expert_ids.reshape(1, tok * top), experts)
    digits = jnp.stack([count // 64, count % 64]).astype(jnp.bfloat16)
    packed = jnp.concatenate(
        [
            cotangent,
            expert_ids.astype(jnp.bfloat16),
            weighted,
            jnp.broadcast_to(digits, (tok, 2)),
            rank_own.reshape(tok, top).astype(jnp.bfloat16),
        ],
        axis=1,
    )
    got = lax.all_gather(packed, "grp")
    dig = got[:, 0, width + 2 * top : width + 2 * top + 2].astype(jnp.float32)
    total = jnp.sum(dig[:, 0] * 64.0 + dig[:, 1])
    scale = LOSS_SCALE / total

    pick_a, dy_a, gate_a, hid_a = dispatch(
        expert_ids.reshape(1, tok * top), rank_own, weighted.reshape(-1), cotangent,
        hidden.reshape(tok * top, ffw), exp_dev, most, n_exp,
    )
    gate_fa = gate_a.reshape(n_exp, exp_dev, most).astype(jnp.float32)
    dy_fa = dy_a.reshape(n_exp, exp_dev, most, width)
    scaled = (gate_fa[..., None] * dy_fa.astype(jnp.float32)).astype(jnp.bfloat16)
    partial_grad = (
        jnp.einsum(
            "sjmgf,sjmd->gjfd",
            hid_a.reshape(n_exp, exp_dev, most, n_grp, f_loc),
            scaled,
            preferred_element_type=jnp.float32,
        )
        * scale
    )
    grad_rows = partial_grad.astype(jnp.bfloat16).reshape(n_grp * exp_dev * f_loc, width)
    d_weight = (
        lax.psum_scatter(grad_rows, "grp", scatter_dimension=0, tiled=True)
        .reshape(exp_dev, f_loc, width)
        .astype(jnp.float32)
    )

    rel = (me + jnp.arange(1, n_grp, dtype=jnp.int32)) % n_grp
    got_b = jnp.take(got, rel, axis=0)
    n_b = n_grp - 1
    pick_b, dy_b, _, _ = dispatch(
        got_b[:, :, width : width + top].astype(jnp.int32).reshape(n_b, tok * top),
        got_b[:, :, width + 2 * top + 2 :].astype(jnp.int32).reshape(n_b, tok * top),
        got_b[:, :, width + top : width + 2 * top].reshape(-1),
        got_b[:, :, :width].reshape(n_b * tok, width),
        None, exp_dev, most, n_exp,
    )

    proj_rel = jnp.concatenate(
        [proj_home(pick_a, dy_a, w_down, 1, most), proj_home(pick_b, dy_b, w_down, n_b, most)]
    ).astype(jnp.bfloat16).reshape(n_grp, tok, top, f_loc)
    back = (jnp.arange(n_grp, dtype=jnp.int32) - me) % n_grp
    proj_slot = jnp.take(proj_rel, back, axis=0)
    proj_got = lax.all_to_all(proj_slot, "grp", split_axis=0, concat_axis=0, tiled=True)
    proj = jnp.transpose(proj_got, (1, 2, 0, 3)).reshape(tok, top, ffw).astype(jnp.float32)

    d_hidden = (weighted.astype(jnp.float32)[..., None] * proj).astype(jnp.bfloat16)
    inner = jnp.sum(hidden.astype(jnp.float32) * proj, axis=2).astype(jnp.bfloat16)
    d_gate = (inner.astype(jnp.float32) * live[:, None]).astype(jnp.bfloat16)
    return (d_hidden, d_gate, d_weight)


def solution(mesh):
    in_specs = (
        P(("grp", "exp"), None),
        P(("grp", "exp"), None, None),
        P(("grp", "exp"), None),
        P(("grp", "exp"), None),
        P("grp"),
        P("exp", "grp", None),
    )
    out_specs = (P(("grp", "exp"), None, None), P(("grp", "exp"), None), P("exp", "grp", None))
    return jax.shard_map(body, mesh=mesh, in_specs=in_specs, out_specs=out_specs, check_vma=False)
```

```python
import jax
import jax.numpy as jnp
from jax import lax
from jax.sharding import PartitionSpec as P

LOSS_SCALE = 32768


def rank_of(ids, experts):
    onehot = (ids[:, :, None] == jnp.arange(experts, dtype=jnp.int32)).astype(jnp.int32)
    return jnp.sum((jnp.cumsum(onehot, axis=1) - onehot) * onehot, axis=2)


def dispatch(ids, rank, wt, cot, hid, exp_dev, most, n_exp):
    n, per = ids.shape
    top = per * n // cot.shape[0]
    rows = n_exp * n * exp_dev * most
    src = jnp.arange(n, dtype=jnp.int32)[:, None]
    target = ((((ids // exp_dev) * n + src) * exp_dev + ids % exp_dev) * most + rank).reshape(-1)
    pick = (target[None, :] == jnp.arange(rows, dtype=jnp.int32)[:, None]).astype(jnp.bfloat16)
    pick_tok = jnp.sum(pick.reshape(rows, n * per // top, top), axis=2)
    per_dest = n * exp_dev * most
    dy_buf = jnp.dot(pick_tok, cot, preferred_element_type=jnp.float32).astype(jnp.bfloat16)
    gate_buf = jnp.dot(pick, wt, preferred_element_type=jnp.float32).astype(jnp.bfloat16)
    dy_r = lax.all_to_all(dy_buf.reshape(n_exp, per_dest, -1), "exp", 0, 0, tiled=True)
    gate_r = lax.all_to_all(gate_buf.reshape(n_exp, per_dest), "exp", 0, 0, tiled=True)
    hid_r = None
    if hid is not None:
        hid_buf = jnp.dot(pick, hid, preferred_element_type=jnp.float32).astype(jnp.bfloat16)
        hid_r = lax.all_to_all(hid_buf.reshape(n_exp, per_dest, -1), "exp", 0, 0, tiled=True)
    return pick, dy_r, gate_r, hid_r


def proj_home(pick, dy_r, w_down, n, most):
    n_exp, exp_dev = dy_r.shape[0], w_down.shape[0]
    dy_r = dy_r.reshape(n_exp, n, exp_dev, most, -1)
    proj = jnp.einsum("cgjmd,jfd->cgjmf", dy_r, w_down, preferred_element_type=jnp.float32)
    back = lax.all_to_all(
        proj.astype(jnp.bfloat16).reshape(n_exp, n * exp_dev * most, -1), "exp", 0, 0, tiled=True
    )
    return jnp.dot(pick.T, back.reshape(-1, back.shape[-1]), preferred_element_type=jnp.float32)


def body(cotangent, hidden, gates, expert_ids, group_counts, w_down):
    tok, top = expert_ids.shape
    ffw = hidden.shape[2]
    width = cotangent.shape[1]
    n_exp = lax.axis_size("exp")
    n_grp = lax.axis_size("grp")
    exp_dev, f_loc = w_down.shape[0], w_down.shape[1]
    experts = exp_dev * n_exp
    most = 5 * tok * top // (4 * experts)
    me = lax.axis_index("grp")

    count = group_counts[0]
    first_row = lax.axis_index("exp") * tok
    live = (first_row + jnp.arange(tok, dtype=jnp.int32) < count).astype(jnp.float32)
    weighted = (gates.astype(jnp.float32) * live[:, None]).astype(jnp.bfloat16)

    rank_own = rank_of(expert_ids.reshape(1, tok * top), experts)
    digits = jnp.stack([count // 64, count % 64]).astype(jnp.bfloat16)
    packed = jnp.concatenate(
        [
            cotangent,
            expert_ids.astype(jnp.bfloat16),
            weighted,
            jnp.broadcast_to(digits, (tok, 2)),
            rank_own.reshape(tok, top).astype(jnp.bfloat16),
        ],
        axis=1,
    )
    got = lax.all_gather(packed, "grp")
    dig = got[:, 0, width + 2 * top : width + 2 * top + 2].astype(jnp.float32)
    total = jnp.sum(dig[:, 0] * 64.0 + dig[:, 1])
    scale = LOSS_SCALE / total

    pick_a, dy_a, gate_a, hid_a = dispatch(
        expert_ids.reshape(1, tok * top), rank_own, weighted.reshape(-1), cotangent,
        hidden.reshape(tok * top, ffw), exp_dev, most, n_exp,
    )
    gate_fa = gate_a.reshape(n_exp, exp_dev, most).astype(jnp.float32)
    dy_fa = dy_a.reshape(n_exp, exp_dev, most, width)
    scaled = (gate_fa[..., None] * dy_fa.astype(jnp.float32)).astype(jnp.bfloat16)
    partial_grad = (
        jnp.einsum(
            "sjmgf,sjmd->jgfd",
            hid_a.reshape(n_exp, exp_dev, most, n_grp, f_loc),
            scaled,
            preferred_element_type=jnp.float32,
        )
        * scale
    )
    grad_rows = partial_grad.astype(jnp.bfloat16).reshape(exp_dev, n_grp * f_loc, width)
    d_weight = jnp.stack(
        [lax.psum_scatter(grad_rows[j], "grp", scatter_dimension=0, tiled=True) for j in range(exp_dev)]
    ).astype(jnp.float32)

    rel = (me + jnp.arange(1, n_grp, dtype=jnp.int32)) % n_grp
    got_b = jnp.take(got, rel, axis=0)
    n_b = n_grp - 1
    pick_b, dy_b, _, _ = dispatch(
        got_b[:, :, width : width + top].astype(jnp.int32).reshape(n_b, tok * top),
        got_b[:, :, width + 2 * top + 2 :].astype(jnp.int32).reshape(n_b, tok * top),
        got_b[:, :, width + top : width + 2 * top].reshape(-1),
        got_b[:, :, :width].reshape(n_b * tok, width),
        None, exp_dev, most, n_exp,
    )

    proj_rel = jnp.concatenate(
        [proj_home(pick_a, dy_a, w_down, 1, most), proj_home(pick_b, dy_b, w_down, n_b, most)]
    ).astype(jnp.bfloat16).reshape(n_grp, tok, top, f_loc)
    back = (jnp.arange(n_grp, dtype=jnp.int32) - me) % n_grp
    proj_slot = jnp.take(proj_rel, back, axis=0)
    proj_got = lax.all_to_all(proj_slot, "grp", split_axis=0, concat_axis=0, tiled=True)
    proj = jnp.transpose(proj_got, (1, 2, 0, 3)).reshape(tok, top, ffw).astype(jnp.float32)

    d_hidden = (weighted.astype(jnp.float32)[..., None] * proj).astype(jnp.bfloat16)
    inner = jnp.sum(hidden.astype(jnp.float32) * proj, axis=2).astype(jnp.bfloat16)
    d_gate = (inner.astype(jnp.float32) * live[:, None]).astype(jnp.bfloat16)
    return (d_hidden, d_gate, d_weight)


def solution(mesh):
    in_specs = (
        P(("grp", "exp"), None),
        P(("grp", "exp"), None, None),
        P(("grp", "exp"), None),
        P(("grp", "exp"), None),
        P("grp"),
        P("exp", "grp", None),
    )
    out_specs = (P(("grp", "exp"), None, None), P(("grp", "exp"), None), P("exp", "grp", None))
    return jax.shard_map(body, mesh=mesh, in_specs=in_specs, out_specs=out_specs, check_vma=False)
```

```python
import jax
import jax.numpy as jnp
from jax import lax
from jax.sharding import PartitionSpec as P

LOSS_SCALE = 32768


def rank_of(ids, experts):
    onehot = (ids[:, :, None] == jnp.arange(experts, dtype=jnp.int32)).astype(jnp.int32)
    return jnp.sum((jnp.cumsum(onehot, axis=1) - onehot) * onehot, axis=2)


def dispatch(ids, rank, wt, cot, hid, exp_dev, most, n_exp, gather_rows=False):
    n, per = ids.shape
    top = per * n // cot.shape[0]
    rows = n_exp * n * exp_dev * most
    src = jnp.arange(n, dtype=jnp.int32)[:, None]
    target = ((((ids // exp_dev) * n + src) * exp_dev + ids % exp_dev) * most + rank).reshape(-1)
    pick = (target[None, :] == jnp.arange(rows, dtype=jnp.int32)[:, None]).astype(jnp.bfloat16)
    pick_tok = jnp.sum(pick.reshape(rows, n * per // top, top), axis=2)
    per_dest = n * exp_dev * most
    if gather_rows:
        tok_ids = jnp.arange(pick_tok.shape[1], dtype=jnp.float32)
        row_tok = jnp.dot(pick_tok.astype(jnp.float32), tok_ids, precision=lax.Precision.HIGHEST)
        dy_buf = jnp.take(cot, row_tok.astype(jnp.int32), axis=0)
    else:
        dy_buf = jnp.dot(pick_tok, cot, preferred_element_type=jnp.float32).astype(jnp.bfloat16)
    gate_buf = jnp.dot(pick, wt, preferred_element_type=jnp.float32).astype(jnp.bfloat16)
    dy_r = lax.all_to_all(dy_buf.reshape(n_exp, per_dest, -1), "exp", 0, 0, tiled=True)
    gate_r = lax.all_to_all(gate_buf.reshape(n_exp, per_dest), "exp", 0, 0, tiled=True)
    hid_r = None
    if hid is not None:
        hid_buf = jnp.dot(pick, hid, preferred_element_type=jnp.float32).astype(jnp.bfloat16)
        hid_r = lax.all_to_all(hid_buf.reshape(n_exp, per_dest, -1), "exp", 0, 0, tiled=True)
    return pick, dy_r, gate_r, hid_r


def proj_home(pick, dy_r, w_down, n, most):
    n_exp, exp_dev = dy_r.shape[0], w_down.shape[0]
    dy_r = dy_r.reshape(n_exp, n, exp_dev, most, -1)
    proj = jnp.einsum("cgjmd,jfd->cgjmf", dy_r, w_down, preferred_element_type=jnp.float32)
    back = lax.all_to_all(
        proj.astype(jnp.bfloat16).reshape(n_exp, n * exp_dev * most, -1), "exp", 0, 0, tiled=True
    )
    return jnp.dot(pick.T, back.reshape(-1, back.shape[-1]), preferred_element_type=jnp.float32)


def body(cotangent, hidden, gates, expert_ids, group_counts, w_down):
    tok, top = expert_ids.shape
    ffw = hidden.shape[2]
    width = cotangent.shape[1]
    n_exp = lax.axis_size("exp")
    n_grp = lax.axis_size("grp")
    exp_dev, f_loc = w_down.shape[0], w_down.shape[1]
    experts = exp_dev * n_exp
    most = 5 * tok * top // (4 * experts)
    me = lax.axis_index("grp")

    count = group_counts[0]
    first_row = lax.axis_index("exp") * tok
    live = (first_row + jnp.arange(tok, dtype=jnp.int32) < count).astype(jnp.float32)
    weighted = (gates.astype(jnp.float32) * live[:, None]).astype(jnp.bfloat16)

    rank_own = rank_of(expert_ids.reshape(1, tok * top), experts)
    digits = jnp.stack([count // 64, count % 64]).astype(jnp.bfloat16)
    packed = jnp.concatenate(
        [
            cotangent,
            expert_ids.astype(jnp.bfloat16),
            weighted,
            jnp.broadcast_to(digits, (tok, 2)),
            rank_own.reshape(tok, top).astype(jnp.bfloat16),
        ],
        axis=1,
    )
    got = lax.all_gather(packed, "grp")
    dig = got[:, 0, width + 2 * top : width + 2 * top + 2].astype(jnp.float32)
    total = jnp.sum(dig[:, 0] * 64.0 + dig[:, 1])
    scale = LOSS_SCALE / total

    pick_a, dy_a, gate_a, hid_a = dispatch(
        expert_ids.reshape(1, tok * top), rank_own, weighted.reshape(-1), cotangent,
        hidden.reshape(tok * top, ffw), exp_dev, most, n_exp,
    )
    gate_fa = gate_a.reshape(n_exp, exp_dev, most).astype(jnp.float32)
    dy_fa = dy_a.reshape(n_exp, exp_dev, most, width)
    scaled = (gate_fa[..., None] * dy_fa.astype(jnp.float32)).astype(jnp.bfloat16)
    partial_grad = (
        jnp.einsum(
            "sjmgf,sjmd->jgfd",
            hid_a.reshape(n_exp, exp_dev, most, n_grp, f_loc),
            scaled,
            preferred_element_type=jnp.float32,
        )
        * scale
    )
    grad_rows = partial_grad.astype(jnp.bfloat16).reshape(exp_dev, n_grp * f_loc, width)
    d_weight = jnp.stack(
        [lax.psum_scatter(grad_rows[j], "grp", scatter_dimension=0, tiled=True) for j in range(exp_dev)]
    ).astype(jnp.float32)

    rel = (me + jnp.arange(1, n_grp, dtype=jnp.int32)) % n_grp
    got_b = jnp.take(got, rel, axis=0)
    n_b = n_grp - 1
    pick_b, dy_b, _, _ = dispatch(
        got_b[:, :, width : width + top].astype(jnp.int32).reshape(n_b, tok * top),
        got_b[:, :, width + 2 * top + 2 :].astype(jnp.int32).reshape(n_b, tok * top),
        got_b[:, :, width + top : width + 2 * top].reshape(-1),
        got_b[:, :, :width].reshape(n_b * tok, width),
        None, exp_dev, most, n_exp, gather_rows=True,
    )

    proj_rel = jnp.concatenate(
        [proj_home(pick_a, dy_a, w_down, 1, most), proj_home(pick_b, dy_b, w_down, n_b, most)]
    ).astype(jnp.bfloat16).reshape(n_grp, tok, top, f_loc)
    back = (jnp.arange(n_grp, dtype=jnp.int32) - me) % n_grp
    proj_slot = jnp.take(proj_rel, back, axis=0)
    proj_got = lax.all_to_all(proj_slot, "grp", split_axis=0, concat_axis=0, tiled=True)
    proj = jnp.transpose(proj_got, (1, 2, 0, 3)).reshape(tok, top, ffw).astype(jnp.float32)

    d_hidden = (weighted.astype(jnp.float32)[..., None] * proj).astype(jnp.bfloat16)
    inner = jnp.sum(hidden.astype(jnp.float32) * proj, axis=2).astype(jnp.bfloat16)
    d_gate = (inner.astype(jnp.float32) * live[:, None]).astype(jnp.bfloat16)
    return (d_hidden, d_gate, d_weight)


def solution(mesh):
    in_specs = (
        P(("grp", "exp"), None),
        P(("grp", "exp"), None, None),
        P(("grp", "exp"), None),
        P(("grp", "exp"), None),
        P("grp"),
        P("exp", "grp", None),
    )
    out_specs = (P(("grp", "exp"), None, None), P(("grp", "exp"), None), P("exp", "grp", None))
    return jax.shard_map(body, mesh=mesh, in_specs=in_specs, out_specs=out_specs, check_vma=False)
```

```python
import jax
import jax.numpy as jnp
from jax import lax
from jax.sharding import PartitionSpec as P

LOSS_SCALE = 32768


def rank_of(ids, experts):
    onehot = (ids[:, :, None] == jnp.arange(experts, dtype=jnp.int32)).astype(jnp.int32)
    return jnp.sum((jnp.cumsum(onehot, axis=1) - onehot) * onehot, axis=2)


def dispatch(ids, rank, wt, cot, hid, exp_dev, most, n_exp):
    n, per = ids.shape
    top = per * n // cot.shape[0]
    rows = n_exp * n * exp_dev * most
    src = jnp.arange(n, dtype=jnp.int32)[:, None]
    target = ((((ids // exp_dev) * n + src) * exp_dev + ids % exp_dev) * most + rank).reshape(-1)
    pick = (target[None, :] == jnp.arange(rows, dtype=jnp.int32)[:, None]).astype(jnp.bfloat16)
    pick_tok = jnp.sum(pick.reshape(rows, n * per // top, top), axis=2)
    per_dest = n * exp_dev * most
    dy_buf = jnp.dot(pick_tok, cot, preferred_element_type=jnp.float32).astype(jnp.bfloat16)
    gate_buf = jnp.dot(pick, wt, preferred_element_type=jnp.float32).astype(jnp.bfloat16)
    dy_r = lax.all_to_all(dy_buf.reshape(n_exp, per_dest, -1), "exp", 0, 0, tiled=True)
    gate_r = lax.all_to_all(gate_buf.reshape(n_exp, per_dest), "exp", 0, 0, tiled=True)
    hid_r = None
    if hid is not None:
        hid_buf = jnp.dot(pick, hid, preferred_element_type=jnp.float32).astype(jnp.bfloat16)
        hid_r = lax.all_to_all(hid_buf.reshape(n_exp, per_dest, -1), "exp", 0, 0, tiled=True)
    return pick, dy_r, gate_r, hid_r


def proj_home(pick, dy_r, w_down, n, most):
    n_exp, exp_dev = dy_r.shape[0], w_down.shape[0]
    dy_r = dy_r.reshape(n_exp, n, exp_dev, most, -1)
    proj = jnp.einsum("cgjmd,jfd->cgjmf", dy_r, w_down, preferred_element_type=jnp.float32)
    back = lax.all_to_all(
        proj.astype(jnp.bfloat16).reshape(n_exp, n * exp_dev * most, -1), "exp", 0, 0, tiled=True
    )
    return jnp.dot(pick.T, back.reshape(-1, back.shape[-1]), preferred_element_type=jnp.float32)


def body(cotangent, hidden, gates, expert_ids, group_counts, w_down):
    tok, top = expert_ids.shape
    ffw = hidden.shape[2]
    width = cotangent.shape[1]
    n_exp = lax.axis_size("exp")
    n_grp = lax.axis_size("grp")
    exp_dev, f_loc = w_down.shape[0], w_down.shape[1]
    experts = exp_dev * n_exp
    most = 5 * tok * top // (4 * experts)
    me = lax.axis_index("grp")

    count = group_counts[0]
    first_row = lax.axis_index("exp") * tok
    live = (first_row + jnp.arange(tok, dtype=jnp.int32) < count).astype(jnp.float32)
    weighted = (gates.astype(jnp.float32) * live[:, None]).astype(jnp.bfloat16)

    rank_own = rank_of(expert_ids.reshape(1, tok * top), experts)
    digits = jnp.stack([count // 64, count % 64]).astype(jnp.bfloat16)
    packed = jnp.concatenate(
        [
            cotangent,
            expert_ids.astype(jnp.bfloat16),
            weighted,
            jnp.broadcast_to(digits, (tok, 2)),
            rank_own.reshape(tok, top).astype(jnp.bfloat16),
        ],
        axis=1,
    )
    got = lax.all_gather(packed, "grp")
    dig = got[:, 0, width + 2 * top : width + 2 * top + 2].astype(jnp.float32)
    total = jnp.sum(dig[:, 0] * 64.0 + dig[:, 1])
    scale = LOSS_SCALE / total

    pick_a, dy_a, gate_a, hid_a = dispatch(
        expert_ids.reshape(1, tok * top), rank_own, weighted.reshape(-1), cotangent,
        hidden.reshape(tok * top, ffw), exp_dev, most, n_exp,
    )
    gate_fa = gate_a.reshape(n_exp, exp_dev, most).astype(jnp.float32)
    dy_fa = dy_a.reshape(n_exp, exp_dev, most, width)
    scaled = (gate_fa[..., None] * dy_fa.astype(jnp.float32)).astype(jnp.bfloat16)
    partial_grad = (
        jnp.einsum(
            "sjmgf,sjmd->jgfd",
            hid_a.reshape(n_exp, exp_dev, most, n_grp, f_loc),
            scaled,
            preferred_element_type=jnp.float32,
        )
        * scale
    )
    grad_rows = partial_grad.astype(jnp.bfloat16).reshape(exp_dev, n_grp * f_loc, width)
    d_weight = jnp.stack(
        [lax.psum_scatter(grad_rows[j], "grp", scatter_dimension=0, tiled=True) for j in range(exp_dev)]
    ).astype(jnp.float32)

    rel = (me + jnp.arange(1, n_grp, dtype=jnp.int32)) % n_grp
    got_b = jnp.take(got, rel, axis=0)
    n_b = n_grp - 1
    pick_b, dy_b, _, _ = dispatch(
        got_b[:, :, width : width + top].astype(jnp.int32).reshape(n_b, tok * top),
        got_b[:, :, width + 2 * top + 2 :].astype(jnp.int32).reshape(n_b, tok * top),
        got_b[:, :, width + top : width + 2 * top].reshape(-1),
        got_b[:, :, :width].reshape(n_b * tok, width),
        None, exp_dev, most, n_exp,
    )

    proj_rel = jnp.concatenate(
        [proj_home(pick_a, dy_a, w_down, 1, most), proj_home(pick_b, dy_b, w_down, n_b, most)]
    ).astype(jnp.bfloat16).reshape(n_grp, tok, top, f_loc)
    proj_slot = jnp.stack(
        [
            sum(
                jnp.where((a - me) % n_grp == i, proj_rel[i], jnp.zeros((), proj_rel.dtype))
                for i in range(n_grp)
            )
            for a in range(n_grp)
        ]
    )
    proj_got = lax.all_to_all(proj_slot, "grp", split_axis=0, concat_axis=0, tiled=True)
    proj = jnp.transpose(proj_got, (1, 2, 0, 3)).reshape(tok, top, ffw).astype(jnp.float32)

    d_hidden = (weighted.astype(jnp.float32)[..., None] * proj).astype(jnp.bfloat16)
    inner = jnp.sum(hidden.astype(jnp.float32) * proj, axis=2).astype(jnp.bfloat16)
    d_gate = (inner.astype(jnp.float32) * live[:, None]).astype(jnp.bfloat16)
    return (d_hidden, d_gate, d_weight)


def solution(mesh):
    in_specs = (
        P(("grp", "exp"), None),
        P(("grp", "exp"), None, None),
        P(("grp", "exp"), None),
        P(("grp", "exp"), None),
        P("grp"),
        P("exp", "grp", None),
    )
    out_specs = (P(("grp", "exp"), None, None), P(("grp", "exp"), None), P("exp", "grp", None))
    return jax.shard_map(body, mesh=mesh, in_specs=in_specs, out_specs=out_specs, check_vma=False)
```
